256 devices in a mesh: rot: 8 (over x_hi, y), space: 32 (over x_lo, z, core).
Axes of the slice: x: 4 (x_hi: 2, x_lo: 2; x = x_hi * 2 + x_lo), y: 4, z: 8, core: 2. Of those that a mesh axis runs over, the one named last changes fastest.
Arguments:
- raster: bfloat16 [4, 512, 2, 256], P(None, 'space'), may hold values from -6 to 6
- coarse_features: bfloat16 [8, 64, 512, 2, 256], P('rot', None, 'space'), may hold values from -6 to 6
- lift_weight: bfloat16 [8, 9, 64, 4], P('rot'), may hold values from -1 to 1
- lift_bias: float32 [64], replicated, may hold values from -3 to 3
- group_weight: bfloat16 [8, 9, 64, 64], P('rot'), may hold values from -0.09375 to 0.09375
- group_bias: float32 [64], replicated, may hold values from -3 to 3
Outputs:
- features: bfloat16 [8, 64, 512, 2, 256], P('rot', None, 'space')
The draws below stay inside these ranges and needn't reach their ends.
All inputs are finite; a program needn't handle non-finite values.
Results may differ from the reference program's by a relative error of at most 0.0045.
Values may be sent and summed in bfloat16 or wider, within the bound.
No kernel may reach another device: no remote copies, remote signals or barrier semaphores. Data moves between devices by JAX's collectives and lax.ppermute only.
A program may use at most 192 MiB of HBM per device.

```python
import jax
import jax.numpy as jnp
import numpy as np
from jax import lax

C = 64
CIN = 4
COLS = 256
TILES = 2
ROTS = 8
HEIGHT = 512


def block_scale(rng, extent, cuts, smallest, top_value):
    def one(axis_at, shards_of):
        draws = jax.random.uniform(jax.random.fold_in(jax.random.fold_in(rng, 6), axis_at), (shards_of,), jnp.float32, smallest / len(cuts), top_value / len(cuts))
        return jnp.repeat(jnp.exp(draws), extent[axis_at] // shards_of).reshape((-1,) + (1,) * (len(extent) - axis_at - 1))

    loudness = one(*cuts[0])
    for cut in cuts[1:]:
        loudness = loudness * one(*cut)
    return loudness


def gaussian(key, shape, deviation, most, split=(), dtype=jnp.bfloat16):
    gain = block_scale(key, shape, split, -0.22, 0.18) if split else 1.0
    result = jax.random.normal(key, shape, jnp.float32) * deviation * gain
    return jnp.minimum(jnp.maximum(result, -most), most).astype(dtype)


def setup_inputs(seed: int = 0) -> dict:
    key_of = jax.random.split(jax.random.key(seed), 7)
    return {
        "raster": gaussian(key_of[0], (CIN, HEIGHT, TILES, COLS), 1.0, 6.0, ((1, 32),)),
        "coarse_features": gaussian(key_of[1], (ROTS, C, HEIGHT, TILES, COLS), 1.0, 6.0, ((0, 8), (2, 32))),
        "lift_weight": gaussian(key_of[2], (ROTS, 9, C, CIN), (9 * CIN) ** -0.5, 1.0, ((0, 8),)),
        "lift_bias": gaussian(key_of[3], (C,), 0.5, 3.0, (), jnp.float32),
        "group_weight": gaussian(key_of[4], (ROTS, 9, C, C), (9 * C * ROTS) ** -0.5, 0.09375, ((0, 8),)),
        "group_bias": gaussian(key_of[5], (C,), 0.5, 3.0, (), jnp.float32),
    }


def conv_full(images, kernel):
    return lax.conv_general_dilated(images, kernel, (1, 1), ((1, 1), (1, 1)), dimension_numbers=("NCHW", "OIHW", "NCHW"), precision=lax.Precision.HIGHEST)


def reference(raster, coarse_features, lift_weight, lift_bias, group_weight, group_bias):
    rotations = lift_weight.shape[0]
    channels = lift_weight.shape[2]
    images = jnp.transpose(raster.astype(jnp.float32), (2, 0, 1, 3))
    tile_count = images.shape[0]
    row_total = images.shape[2]
    col_total = images.shape[3]
    lift_kernel = jnp.transpose(lift_weight.astype(jnp.float32).reshape(rotations, 3, 3, channels, -1), (0, 3, 4, 1, 2)).reshape(rotations * channels, -1, 3, 3)
    lifted = conv_full(images, lift_kernel).reshape(tile_count, rotations, channels, row_total, col_total)
    coarse = jnp.transpose(coarse_features.astype(jnp.float32), (3, 0, 1, 2, 4))
    hidden = jnp.maximum(lifted + lift_bias[None, None, :, None, None] + coarse, 0.0).astype(jnp.bfloat16)
    hidden = lax.optimization_barrier(hidden)
    relative = (np.arange(rotations)[:, None] - np.arange(rotations)[None, :]) % rotations
    filter_bank = group_weight.astype(jnp.float32)[relative]
    filter_bank = filter_bank.reshape(rotations, rotations, 3, 3, channels, channels)
    group_kernel = jnp.transpose(filter_bank, (0, 4, 1, 5, 2, 3)).reshape(rotations * channels, rotations * channels, 3, 3)
    mixed_sum = conv_full(hidden.astype(jnp.float32).reshape(tile_count, rotations * channels, row_total, col_total), group_kernel)
    mixed_sum = mixed_sum.reshape(tile_count, rotations, channels, row_total, col_total) + group_bias[None, None, :, None, None]
    output = jnp.maximum(mixed_sum, 0.0).astype(jnp.bfloat16)
    return jnp.transpose(output, (1, 2, 3, 0, 4))
```

```python
import numpy as np
import jax
import jax.numpy as jnp
from jax import lax
from jax.sharding import PartitionSpec as P


def padded_rows(array, axis, dim, width):
    size, length = lax.axis_size(axis), array.shape[dim]
    up = [(i, i + 1) for i in range(size - 1)]
    down = [(j, i) for i, j in up]
    last = lax.slice_in_dim(array, length - width, length, axis=dim)
    leading = lax.slice_in_dim(array, 0, width, axis=dim)
    before = lax.ppermute(last, axis, up)
    after = lax.ppermute(leading, axis, down)
    return jnp.concatenate([before, array, after], axis=dim)


def conv_rows_valid(images, kernel):
    return lax.conv_general_dilated(
        images,
        kernel,
        (1, 1),
        ((0, 0), (1, 1)),
        dimension_numbers=("CHNW", "HWOI", "CHNW"),
        preferred_element_type=jnp.float32,
    )


def shards(raster, coarse_features, lift_weight, lift_bias, group_weight, group_bias):
    rot_count = lax.axis_size("rot")
    channels = lift_weight.shape[2]
    rows = raster.shape[1]
    chunk = rows // rot_count

    raster_padded = padded_rows(raster, "space", 1, 1)
    lift_kernel = lift_weight[0].reshape(3, 3, channels, -1)
    lifted = conv_rows_valid(raster_padded, lift_kernel)
    lifted = lifted + lift_bias[:, None, None, None] + coarse_features[0].astype(jnp.float32)
    hidden = jnp.maximum(lifted, 0.0).astype(jnp.bfloat16)

    hidden_ext = padded_rows(hidden, "space", 1, 1)
    windows = jnp.stack(
        [lax.slice_in_dim(hidden_ext, k * chunk, k * chunk + chunk + 2, axis=1) for k in range(rot_count)], 0
    )
    gathered = lax.all_to_all(windows, "rot", 0, 0)

    filters = lax.all_gather(group_weight[0], "rot", axis=0)
    relative = (np.arange(rot_count)[:, None] - np.arange(rot_count)[None, :]) % rot_count
    bank = filters[relative]
    bank = bank.reshape(rot_count, rot_count, 3, 3, channels, channels)
    bank = jnp.transpose(bank, (2, 3, 0, 4, 1, 5)).reshape(3, 3, rot_count * channels, rot_count * channels)

    images = gathered.reshape((rot_count * channels,) + gathered.shape[2:])
    mixed = conv_rows_valid(images, bank)
    bias = jnp.tile(group_bias, rot_count)
    mixed = jnp.maximum(mixed + bias[:, None, None, None], 0.0).astype(jnp.bfloat16)
    mixed = mixed.reshape((rot_count, channels) + mixed.shape[1:])

    returned = lax.all_to_all(mixed, "rot", 0, 0)
    result = jnp.transpose(returned, (1, 0, 2, 3, 4)).reshape(
        (channels, rows) + returned.shape[3:]
    )
    return result[None]


def solution(mesh):
    return jax.shard_map(
        shards,
        mesh=mesh,
        in_specs=(
            P(None, "space", None, None),
            P("rot", None, "space", None, None),
            P("rot", None, None, None),
            P(),
            P("rot", None, None, None),
            P(),
        ),
        out_specs=P("rot", None, "space", None, None),
        check_vma=False,
    )
```

```python
import jax
import jax.numpy as jnp
from jax import lax
from jax.sharding import PartitionSpec as P


def padded_rows(array, axis, dim, width):
    size, length = lax.axis_size(axis), array.shape[dim]
    up = [(i, i + 1) for i in range(size - 1)]
    down = [(j, i) for i, j in up]
    last = lax.slice_in_dim(array, length - width, length, axis=dim)
    leading = lax.slice_in_dim(array, 0, width, axis=dim)
    before = lax.ppermute(last, axis, up)
    after = lax.ppermute(leading, axis, down)
    return jnp.concatenate([before, array, after], axis=dim)


def conv_rows_valid(images, kernel):
    return lax.conv_general_dilated(
        images,
        kernel,
        (1, 1),
        ((0, 0), (1, 1)),
        dimension_numbers=("CHNW", "HWOI", "CHNW"),
        preferred_element_type=jnp.float32,
    )


def shards(raster, coarse_features, lift_weight, lift_bias, group_weight, group_bias):
    rot_count = lax.axis_size("rot")
    channels = lift_weight.shape[2]
    rows = raster.shape[1]
    chunk = rows // rot_count

    raster_padded = padded_rows(raster, "space", 1, 1)
    lift_kernel = lift_weight[0].reshape(3, 3, channels, -1)
    lifted = conv_rows_valid(raster_padded, lift_kernel)
    lifted = lifted + lift_bias[:, None, None, None] + coarse_features[0].astype(jnp.float32)
    hidden = jnp.maximum(lifted, 0.0).astype(jnp.bfloat16)

    hidden_ext = padded_rows(hidden, "space", 1, 1)
    windows = jnp.stack(
        [lax.slice_in_dim(hidden_ext, k * chunk, k * chunk + chunk + 2, axis=1) for k in range(rot_count)], 0
    )
    gathered = lax.all_to_all(windows, "rot", 0, 0)

    spread = jnp.broadcast_to(group_weight, (rot_count,) + group_weight.shape[1:])
    filters = lax.all_to_all(spread, "rot", 0, 0)
    order = [rot_count - 1 - j for j in range(rot_count)] * 2
    doubled = jnp.concatenate([filters[r] for r in order], axis=-1)
    bank = jnp.stack(
        [
            lax.slice_in_dim(doubled, channels * (rot_count - 1 - g), channels * (2 * rot_count - 1 - g), axis=2)
            for g in range(rot_count)
        ],
        1,
    ).reshape(3, 3, rot_count * channels, rot_count * channels)

    images = gathered.reshape((rot_count * channels,) + gathered.shape[2:])
    mixed = conv_rows_valid(images, bank)
    bias = jnp.tile(group_bias, rot_count)
    mixed = jnp.maximum(mixed + bias[:, None, None, None], 0.0).astype(jnp.bfloat16)
    mixed = mixed.reshape((rot_count, channels) + mixed.shape[1:])

    returned = lax.all_to_all(mixed, "rot", 0, 0)
    result = jnp.transpose(returned, (1, 0, 2, 3, 4)).reshape(
        (channels, rows) + returned.shape[3:]
    )
    return result[None]


def solution(mesh):
    return jax.shard_map(
        shards,
        mesh=mesh,
        in_specs=(
            P(None, "space", None, None),
            P("rot", None, "space", None, None),
            P("rot", None, None, None),
            P(),
            P("rot", None, None, None),
            P(),
        ),
        out_specs=P("rot", None, "space", None, None),
        check_vma=False,
    )
```

```python
import jax
import jax.numpy as jnp
from jax import lax
from jax.experimental import pallas as pl
from jax.sharding import PartitionSpec as P


def padded_rows(array, axis, dim, width):
    size, length = lax.axis_size(axis), array.shape[dim]
    up = [(i, i + 1) for i in range(size - 1)]
    down = [(j, i) for i, j in up]
    last = lax.slice_in_dim(array, length - width, length, axis=dim)
    leading = lax.slice_in_dim(array, 0, width, axis=dim)
    before = lax.ppermute(last, axis, up)
    after = lax.ppermute(leading, axis, down)
    return jnp.concatenate([before, array, after], axis=dim)


def passed_along(array, axis, by):
    size = lax.axis_size(axis)
    return lax.ppermute(array, axis, [(i, (i + by) % size) for i in range(size)])


def conv_rows_valid(images, kernel):
    return lax.conv_general_dilated(
        images,
        kernel,
        (1, 1),
        ((0, 0), (1, 1)),
        dimension_numbers=("CHNW", "HWOI", "CHNW"),
        preferred_element_type=jnp.float32,
    )


def bank_kernel(pairs_ref, bank_ref):
    count, _, channels, lanes = pairs_ref.shape
    for g in range(count):
        for p in range(bank_ref.shape[2] // lanes):
            bank_ref[:, g * channels : (g + 1) * channels, p * lanes : (p + 1) * lanes] = pairs_ref[
                (g + 2 * p) % count
            ]


def circulant_bank(filters):
    count, taps, channels, _ = filters.shape
    pairs = jnp.concatenate([filters, jnp.roll(filters, -1, axis=0)], axis=-1)
    bank = pl.pallas_call(
        bank_kernel,
        out_shape=jax.ShapeDtypeStruct((taps, count * channels, count * channels), filters.dtype),
    )(pairs)
    return bank.reshape(3, 3, count * channels, count * channels)


def shards(raster, coarse_features, lift_weight, lift_bias, group_weight, group_bias):
    n = lax.axis_size("rot")
    me = lax.axis_index("rot")
    channels = lift_weight.shape[2]
    rows = raster.shape[1]
    chunk = rows // n

    own_filter = group_weight[0]
    came = jnp.stack([own_filter] + [passed_along(own_filter, "rot", d) for d in range(1, n)])
    backwards = came[jnp.array([(-j) % n for j in range(n)])]
    filters = jnp.roll(backwards, me, axis=0)

    raster_padded = padded_rows(raster, "space", 1, 1)
    lift_kernel = lift_weight[0].reshape(3, 3, channels, -1)
    lifted = conv_rows_valid(raster_padded, lift_kernel)
    lifted = lifted + lift_bias[:, None, None, None] + coarse_features[0].astype(jnp.float32)
    hidden = jnp.maximum(lifted, 0.0).astype(jnp.bfloat16)

    hidden_ext = padded_rows(hidden, "space", 1, 1)
    split = (channels, n, chunk) + hidden.shape[2:]
    top = lax.slice_in_dim(hidden_ext, 0, rows, axis=1).reshape(split)
    bottom = lax.slice_in_dim(hidden_ext, 2, rows + 2, axis=1).reshape(split)
    windows = jnp.concatenate([top, lax.slice_in_dim(bottom, chunk - 2, chunk, axis=2)], axis=2)
    windows = jnp.transpose(windows, (1, 0, 2, 3, 4))

    incoming = [windows[me]]
    for d in range(1, n):
        outgoing = lax.dynamic_index_in_dim(windows, (me + d) % n, 0, keepdims=False)
        incoming.append(passed_along(outgoing, "rot", d))
    images = jnp.stack(incoming).reshape((n * channels,) + windows.shape[2:])

    mixed = conv_rows_valid(images, circulant_bank(filters))
    bias = jnp.tile(group_bias, n)
    mixed = jnp.maximum(mixed + bias[:, None, None, None], 0.0).astype(jnp.bfloat16)
    mixed = mixed.reshape((n, channels) + mixed.shape[1:])

    returned = [mixed[0]] + [passed_along(mixed[j], "rot", j) for j in range(1, n)]
    backwards = jnp.stack([returned[(-j) % n] for j in range(n)])
    chunks = jnp.roll(backwards, me, axis=0)
    result = jnp.transpose(chunks, (1, 0, 2, 3, 4)).reshape((channels, rows) + chunks.shape[3:])
    return result[None]


def solution(mesh):
    return jax.shard_map(
        shards,
        mesh=mesh,
        in_specs=(
            P(None, "space", None, None),
            P("rot", None, "space", None, None),
            P("rot", None, None, None),
            P(),
            P("rot", None, None, None),
            P(),
        ),
        out_specs=P("rot", None, "space", None, None),
        check_vma=False,
    )
```

```python
import jax
import jax.numpy as jnp
from jax import lax
from jax.experimental import pallas as pl
from jax.experimental.pallas import tpu as pltpu
from jax.sharding import PartitionSpec as P


def padded_rows(array, axis, dim, width):
    size, length = lax.axis_size(axis), array.shape[dim]
    up = [(i, i + 1) for i in range(size - 1)]
    down = [(j, i) for i, j in up]
    last = lax.slice_in_dim(array, length - width, length, axis=dim)
    leading = lax.slice_in_dim(array, 0, width, axis=dim)
    before = lax.ppermute(last, axis, up)
    after = lax.ppermute(leading, axis, down)
    return jnp.concatenate([before, array, after], axis=dim)


def conv_rows_valid(images, kernel):
    return lax.conv_general_dilated(
        images,
        kernel,
        (1, 1),
        ((0, 0), (1, 1)),
        dimension_numbers=("CHNW", "HWOI", "CHNW"),
        preferred_element_type=jnp.float32,
    )


def bank_kernel(pairs_ref, bank_ref):
    count, _, channels, lanes = pairs_ref.shape
    for g in range(count):
        for p in range(bank_ref.shape[2] // lanes):
            bank_ref[:, g * channels : (g + 1) * channels, p * lanes : (p + 1) * lanes] = pairs_ref[
                (g - 2 * p) % count
            ]


def circulant_bank(filters):
    count, taps, channels, _ = filters.shape
    pairs = jnp.concatenate([filters, jnp.roll(filters, 1, axis=0)], axis=-1)
    return pl.pallas_call(
        bank_kernel,
        out_shape=jax.ShapeDtypeStruct((taps, count * channels, count * channels), filters.dtype),
    )(pairs)


def mixing_kernel(bank_ref, bias_ref, x_ref, o_ref):
    row, tile = pl.program_id(0), pl.program_id(1)
    count, channels, cols = x_ref.shape[0], x_ref.shape[3], x_ref.shape[4]
    planes = [
        jnp.concatenate([x_ref[h, row + dy, tile] for h in range(count)], axis=0) for dy in range(3)
    ]
    sums = []
    for dx in range(3):
        total = None
        for dy in range(3):
            term = jnp.dot(bank_ref[3 * dy + dx], planes[dy], preferred_element_type=jnp.float32)
            total = term if total is None else total + term
        sums.append(total)
    column = lax.broadcasted_iota(jnp.int32, sums[0].shape, 1)
    left = jnp.where(column == 0, 0.0, pltpu.roll(sums[0], 1, 1))
    right = jnp.where(column == cols - 1, 0.0, pltpu.roll(sums[2], cols - 1, 1))
    mixed = sums[1] + left + right + bias_ref[...]
    mixed = jnp.maximum(mixed, 0.0).astype(o_ref.dtype)
    for g in range(count):
        o_ref[g, 0, 0] = mixed[g * channels : (g + 1) * channels]


def group_mix(bank, bias, windows):
    count, rows_in, tiles, channels, cols = windows.shape
    rows_out = rows_in - 2
    full = count * channels
    return pl.pallas_call(
        mixing_kernel,
        grid=(rows_out, tiles),
        in_specs=[
            pl.BlockSpec((9, full, full), lambda r, t: (0, 0, 0)),
            pl.BlockSpec((full, 1), lambda r, t: (0, 0)),
            pl.BlockSpec(windows.shape, lambda r, t: (0, 0, 0, 0, 0)),
        ],
        out_specs=pl.BlockSpec((count, 1, 1, channels, cols), lambda r, t: (0, r, t, 0, 0)),
        out_shape=jax.ShapeDtypeStruct((count, rows_out, tiles, channels, cols), jnp.bfloat16),
        compiler_params=pltpu.CompilerParams(vmem_limit_bytes=48 * 1024 * 1024),
    )(bank, bias, windows)


def shards(raster, coarse_features, lift_weight, lift_bias, group_weight, group_bias):
    n = lax.axis_size("rot")
    channels = lift_weight.shape[2]
    rows = raster.shape[1]
    chunk = rows // n

    raster_padded = padded_rows(raster, "space", 1, 1)
    lift_kernel = lift_weight[0].reshape(3, 3, channels, -1)
    lifted = conv_rows_valid(raster_padded, lift_kernel)
    lifted = lifted + lift_bias[:, None, None, None] + coarse_features[0].astype(jnp.float32)
    hidden = jnp.maximum(lifted, 0.0).astype(jnp.bfloat16)

    hidden_ext = jnp.transpose(padded_rows(hidden, "space", 1, 1), (1, 2, 0, 3))
    split = (n, chunk) + hidden_ext.shape[1:]
    top = lax.slice_in_dim(hidden_ext, 0, rows, axis=0).reshape(split)
    bottom = lax.slice_in_dim(hidden_ext, 2, rows + 2, axis=0).reshape(split)
    windows = jnp.concatenate([top, lax.slice_in_dim(bottom, chunk - 2, chunk, axis=1)], axis=1)
    gathered = lax.all_to_all(windows, "rot", 0, 0)

    spread = jnp.broadcast_to(group_weight, (n,) + group_weight.shape[1:])
    filters = lax.all_to_all(spread, "rot", 0, 0)
    bias = jnp.tile(group_bias, n)[:, None]
    mixed = group_mix(circulant_bank(filters), bias, gathered)

    returned = lax.all_to_all(mixed, "rot", 0, 0)
    result = jnp.transpose(returned, (3, 0, 1, 2, 4)).reshape((channels, rows) + returned.shape[2:3] + returned.shape[4:])
    return result[None]


def solution(mesh):
    return jax.shard_map(
        shards,
        mesh=mesh,
        in_specs=(
            P(None, "space", None, None),
            P("rot", None, "space", None, None),
            P("rot", None, None, None),
            P(),
            P("rot", None, None, None),
            P(),
        ),
        out_specs=P("rot", None, "space", None, None),
        check_vma=False,
    )
```

```python
import jax
import jax.numpy as jnp
from jax import lax
from jax.experimental import pallas as pl
from jax.experimental.pallas import tpu as pltpu
from jax.sharding import PartitionSpec as P


def padded_rows(array, axis, dim, width):
    size, length = lax.axis_size(axis), array.shape[dim]
    up = [(i, i + 1) for i in range(size - 1)]
    down = [(j, i) for i, j in up]
    last = lax.slice_in_dim(array, length - width, length, axis=dim)
    leading = lax.slice_in_dim(array, 0, width, axis=dim)
    before = lax.ppermute(last, axis, up)
    after = lax.ppermute(leading, axis, down)
    return jnp.concatenate([before, array, after], axis=dim)


def bank_kernel(pairs_ref, bank_ref):
    count, _, channels, lanes = pairs_ref.shape
    for g in range(count):
        for p in range(bank_ref.shape[2] // lanes):
            bank_ref[:, g * channels : (g + 1) * channels, p * lanes : (p + 1) * lanes] = pairs_ref[
                (g - 2 * p) % count
            ]


def circulant_bank(filters):
    count, taps, channels, _ = filters.shape
    pairs = jnp.concatenate([filters, jnp.roll(filters, 1, axis=0)], axis=-1)
    return pl.pallas_call(
        bank_kernel,
        out_shape=jax.ShapeDtypeStruct((taps, count * channels, count * channels), filters.dtype),
    )(pairs)


def mixing_kernel(bank_ref, bias_ref, x_ref, o_ref):
    row, tile = pl.program_id(0), pl.program_id(1)
    count, channels, cols = x_ref.shape[0], x_ref.shape[3], x_ref.shape[4]
    planes = [
        jnp.concatenate([x_ref[h, row + dy, tile] for h in range(count)], axis=0) for dy in range(3)
    ]
    sums = []
    for dx in range(3):
        total = None
        for dy in range(3):
            term = jnp.dot(bank_ref[3 * dy + dx], planes[dy], preferred_element_type=jnp.float32)
            total = term if total is None else total + term
        sums.append(total)
    column = lax.broadcasted_iota(jnp.int32, sums[0].shape, 1)
    left = jnp.where(column == 0, 0.0, pltpu.roll(sums[0], 1, 1))
    right = jnp.where(column == cols - 1, 0.0, pltpu.roll(sums[2], cols - 1, 1))
    mixed = sums[1] + left + right + bias_ref[...]
    mixed = jnp.maximum(mixed, 0.0).astype(o_ref.dtype)
    for g in range(count):
        o_ref[g, 0, 0] = mixed[g * channels : (g + 1) * channels]


def group_mix(bank, bias, windows):
    count, rows_in, tiles, channels, cols = windows.shape
    rows_out = rows_in - 2
    full = count * channels
    return pl.pallas_call(
        mixing_kernel,
        grid=(rows_out, tiles),
        in_specs=[
            pl.BlockSpec((9, full, full), lambda r, t: (0, 0, 0)),
            pl.BlockSpec((full, 1), lambda r, t: (0, 0)),
            pl.BlockSpec(windows.shape, lambda r, t: (0, 0, 0, 0, 0)),
        ],
        out_specs=pl.BlockSpec((count, 1, 1, channels, cols), lambda r, t: (0, r, t, 0, 0)),
        out_shape=jax.ShapeDtypeStruct((count, rows_out, tiles, channels, cols), jnp.bfloat16),
        compiler_params=pltpu.CompilerParams(vmem_limit_bytes=48 * 1024 * 1024),
    )(bank, bias, windows)


def shards(raster, coarse_features, lift_weight, lift_bias, group_weight, group_bias):
    n = lax.axis_size("rot")
    channels = lift_weight.shape[2]
    rows = raster.shape[1]
    chunk = rows // n

    raster_padded = jnp.pad(padded_rows(raster, "space", 1, 1), ((0, 0), (0, 0), (0, 0), (1, 1)))
    cols = raster.shape[3]
    taps = jnp.stack(
        [raster_padded[:, dy : dy + rows, :, dx : dx + cols] for dy in range(3) for dx in range(3)], 0
    ).reshape((-1,) + raster.shape[1:])
    lift_matrix = jnp.transpose(lift_weight[0], (1, 0, 2)).reshape(channels, -1)
    lifted = jnp.einsum("ok,krtw->rtow", lift_matrix, taps, preferred_element_type=jnp.float32)
    coarse = jnp.transpose(coarse_features[0], (1, 2, 0, 3)).astype(jnp.float32)
    lifted = lifted + lift_bias[None, None, :, None] + coarse
    hidden = jnp.maximum(lifted, 0.0).astype(jnp.bfloat16)

    hidden_ext = padded_rows(hidden, "space", 0, 1)
    split = (n, chunk) + hidden_ext.shape[1:]
    top = lax.slice_in_dim(hidden_ext, 0, rows, axis=0).reshape(split)
    bottom = lax.slice_in_dim(hidden_ext, 2, rows + 2, axis=0).reshape(split)
    windows = jnp.concatenate([top, lax.slice_in_dim(bottom, chunk - 2, chunk, axis=1)], axis=1)
    gathered = lax.all_to_all(windows, "rot", 0, 0)

    spread = jnp.broadcast_to(group_weight, (n,) + group_weight.shape[1:])
    filters = lax.all_to_all(spread, "rot", 0, 0)
    bias = jnp.tile(group_bias, n)[:, None]
    mixed = group_mix(circulant_bank(filters), bias, gathered)

    returned = lax.all_to_all(mixed, "rot", 0, 0)
    result = jnp.transpose(returned, (3, 0, 1, 2, 4)).reshape((channels, rows) + returned.shape[2:3] + returned.shape[4:])
    return result[None]


def solution(mesh):
    return jax.shard_map(
        shards,
        mesh=mesh,
        in_specs=(
            P(None, "space", None, None),
            P("rot", None, "space", None, None),
            P("rot", None, None, None),
            P(),
            P("rot", None, None, None),
            P(),
        ),
        out_specs=P("rot", None, "space", None, None),
        check_vma=False,
    )
```

```python
import jax
import jax.numpy as jnp
from jax import lax
from jax.experimental import pallas as pl
from jax.experimental.pallas import tpu as pltpu
from jax.sharding import PartitionSpec as P


def padded_rows(array, axis, dim, width):
    size, length = lax.axis_size(axis), array.shape[dim]
    up = [(i, i + 1) for i in range(size - 1)]
    down = [(j, i) for i, j in up]
    last = lax.slice_in_dim(array, length - width, length, axis=dim)
    leading = lax.slice_in_dim(array, 0, width, axis=dim)
    before = lax.ppermute(last, axis, up)
    after = lax.ppermute(leading, axis, down)
    return jnp.concatenate([before, array, after], axis=dim)


def bank_kernel(pairs_ref, bank_ref):
    count, _, channels, lanes = pairs_ref.shape
    for g in range(count):
        for p in range(bank_ref.shape[2] // lanes):
            bank_ref[:, g * channels : (g + 1) * channels, p * lanes : (p + 1) * lanes] = pairs_ref[
                (g - 2 * p) % count
            ]


def circulant_bank(filters):
    count, taps, channels, _ = filters.shape
    pairs = jnp.concatenate([filters, jnp.roll(filters, 1, axis=0)], axis=-1)
    return pl.pallas_call(
        bank_kernel,
        out_shape=jax.ShapeDtypeStruct((taps, count * channels, count * channels), filters.dtype),
    )(pairs)


def mixing_kernel(bank_ref, bias_ref, x_ref, o_ref):
    row = pl.program_id(0)
    count, channels, cols = x_ref.shape[0], x_ref.shape[2], x_ref.shape[3]
    planes = [jnp.concatenate([x_ref[h, row + dy] for h in range(count)], axis=0) for dy in range(3)]
    sums = []
    for dx in range(3):
        total = None
        for dy in range(3):
            term = jnp.dot(bank_ref[3 * dy + dx], planes[dy], preferred_element_type=jnp.float32)
            total = term if total is None else total + term
        sums.append(total)
    column = lax.broadcasted_iota(jnp.int32, sums[0].shape, 1)
    left = jnp.where(column == 0, 0.0, pltpu.roll(sums[0], 1, 1))
    right = jnp.where(column == cols - 1, 0.0, pltpu.roll(sums[2], cols - 1, 1))
    mixed = sums[1] + left + right + bias_ref[...]
    mixed = jnp.maximum(mixed, 0.0).astype(o_ref.dtype)
    for g in range(count):
        o_ref[g, 0] = mixed[g * channels : (g + 1) * channels]


def group_mix(bank, bias, windows):
    count, rows_in, channels, cols = windows.shape
    rows_out = rows_in - 2
    full = count * channels
    return pl.pallas_call(
        mixing_kernel,
        grid=(rows_out,),
        in_specs=[
            pl.BlockSpec((9, full, full), lambda r: (0, 0, 0)),
            pl.BlockSpec((full, 1), lambda r: (0, 0)),
            pl.BlockSpec(windows.shape, lambda r: (0, 0, 0, 0)),
        ],
        out_specs=pl.BlockSpec((count, 1, channels, cols), lambda r: (0, r, 0, 0)),
        out_shape=jax.ShapeDtypeStruct((count, rows_out, channels, cols), jnp.bfloat16),
        compiler_params=pltpu.CompilerParams(vmem_limit_bytes=48 * 1024 * 1024),
    )(bank, bias, windows)


def shards(raster, coarse_features, lift_weight, lift_bias, group_weight, group_bias):
    n = lax.axis_size("rot")
    channels = lift_weight.shape[2]
    rows = raster.shape[1]
    chunk = rows // n

    tiles, cols = raster.shape[2], raster.shape[3]
    quarters = n // tiles
    span = rows // quarters
    space = lax.axis_index("space")

    raster_padded = jnp.pad(padded_rows(raster, "space", 1, 2), ((0, 0), (0, 0), (0, 0), (1, 1)))
    taps = jnp.stack(
        [raster_padded[:, dy : dy + rows + 2, :, dx : dx + cols] for dy in range(3) for dx in range(3)], 0
    ).reshape((-1, rows + 2) + raster.shape[2:])
    lift_matrix = jnp.transpose(lift_weight[0], (1, 0, 2)).reshape(channels, -1)
    lifted = jnp.einsum("ok,krtw->rtow", lift_matrix, taps, preferred_element_type=jnp.float32)
    coarse = jnp.transpose(padded_rows(coarse_features[0], "space", 1, 1), (1, 2, 0, 3))
    lifted = lifted + lift_bias[None, None, :, None] + coarse.astype(jnp.float32)
    line = lax.broadcasted_iota(jnp.int32, (rows + 2, 1, 1, 1), 0)
    inside = ((line > 0) | (space > 0)) & ((line < rows + 1) | (space < lax.axis_size("space") - 1))
    hidden_ext = jnp.where(inside, jnp.maximum(lifted, 0.0), 0.0).astype(jnp.bfloat16)

    split = (quarters, span) + hidden_ext.shape[1:]
    top = lax.slice_in_dim(hidden_ext, 0, rows, axis=0).reshape(split)
    bottom = lax.slice_in_dim(hidden_ext, 2, rows + 2, axis=0).reshape(split)
    windows = jnp.concatenate([top, lax.slice_in_dim(bottom, span - 2, span, axis=1)], axis=1)
    windows = jnp.transpose(windows, (2, 0, 1, 3, 4)).reshape((n, span + 2) + hidden_ext.shape[2:])
    gathered = lax.all_to_all(windows, "rot", 0, 0)

    spread = jnp.broadcast_to(group_weight, (n,) + group_weight.shape[1:])
    filters = lax.all_to_all(spread, "rot", 0, 0)
    bias = jnp.tile(group_bias, n)[:, None]
    mixed = group_mix(circulant_bank(filters), bias, gathered)

    returned = lax.all_to_all(mixed, "rot", 0, 0)
    returned = returned.reshape((tiles, quarters) + returned.shape[1:])
    result = jnp.transpose(returned, (3, 1, 2, 0, 4)).reshape((channels, rows, tiles, cols))
    return result[None]


def solution(mesh):
    return jax.shard_map(
        shards,
        mesh=mesh,
        in_specs=(
            P(None, "space", None, None),
            P("rot", None, "space", None, None),
            P("rot", None, None, None),
            P(),
            P("rot", None, None, None),
            P(),
        ),
        out_specs=P("rot", None, "space", None, None),
        check_vma=False,
    )
```

```python
import jax
import jax.numpy as jnp
from jax import lax
from jax.experimental import pallas as pl
from jax.experimental.pallas import tpu as pltpu
from jax.sharding import PartitionSpec as P


def padded_rows(array, axis, dim, width):
    size, length = lax.axis_size(axis), array.shape[dim]
    up = [(i, i + 1) for i in range(size - 1)]
    down = [(j, i) for i, j in up]
    last = lax.slice_in_dim(array, length - width, length, axis=dim)
    leading = lax.slice_in_dim(array, 0, width, axis=dim)
    before = lax.ppermute(last, axis, up)
    after = lax.ppermute(leading, axis, down)
    return jnp.concatenate([before, array, after], axis=dim)


def bank_kernel(pairs_ref, bank_ref):
    count, _, channels, lanes = pairs_ref.shape
    for g in range(count):
        for p in range(bank_ref.shape[2] // lanes):
            bank_ref[:, g * channels : (g + 1) * channels, p * lanes : (p + 1) * lanes] = pairs_ref[
                (g - 2 * p) % count
            ]


def circulant_bank(filters):
    count, taps, channels, _ = filters.shape
    pairs = jnp.concatenate([filters, jnp.roll(filters, 1, axis=0)], axis=-1)
    return pl.pallas_call(
        bank_kernel,
        out_shape=jax.ShapeDtypeStruct((taps, count * channels, count * channels), filters.dtype),
    )(pairs)


def mixing_kernel(bank_ref, bias_ref, x_ref, o_ref):
    row = pl.program_id(0)
    count, channels, cols = x_ref.shape[0], x_ref.shape[2], x_ref.shape[3]
    planes = [jnp.concatenate([x_ref[h, row + dy] for h in range(count)], axis=0) for dy in range(3)]
    sums = []
    for dx in range(3):
        total = None
        for dy in range(3):
            term = jnp.dot(bank_ref[3 * dy + dx], planes[dy], preferred_element_type=jnp.float32)
            total = term if total is None else total + term
        sums.append(total)
    column = lax.broadcasted_iota(jnp.int32, sums[0].shape, 1)
    left = jnp.where(column == 0, 0.0, pltpu.roll(sums[0], 1, 1))
    right = jnp.where(column == cols - 1, 0.0, pltpu.roll(sums[2], cols - 1, 1))
    mixed = sums[1] + left + right + bias_ref[...]
    mixed = jnp.maximum(mixed, 0.0).astype(o_ref.dtype)
    for g in range(count):
        o_ref[g, 0] = mixed[g * channels : (g + 1) * channels]


def group_mix(bank, bias, windows):
    count, rows_in, channels, cols = windows.shape
    rows_out = rows_in - 2
    full = count * channels
    return pl.pallas_call(
        mixing_kernel,
        grid=(rows_out,),
        in_specs=[
            pl.BlockSpec((9, full, full), lambda r: (0, 0, 0)),
            pl.BlockSpec((full, 1), lambda r: (0, 0)),
            pl.BlockSpec(windows.shape, lambda r: (0, 0, 0, 0)),
        ],
        out_specs=pl.BlockSpec((count, 1, channels, cols), lambda r: (0, r, 0, 0)),
        out_shape=jax.ShapeDtypeStruct((count, rows_out, channels, cols), jnp.bfloat16),
        compiler_params=pltpu.CompilerParams(vmem_limit_bytes=48 * 1024 * 1024),
    )(bank, bias, windows)


def shards(raster, coarse_features, lift_weight, lift_bias, group_weight, group_bias):
    n = lax.axis_size("rot")
    channels = lift_weight.shape[2]
    rows = raster.shape[1]
    chunk = rows // n

    tiles, cols = raster.shape[2], raster.shape[3]
    quarters = n // tiles
    span = rows // quarters
    space = lax.axis_index("space")

    raster_padded = jnp.pad(padded_rows(raster, "space", 1, 2), ((0, 0), (0, 0), (0, 0), (1, 1)))
    lift_matrix = jnp.transpose(lift_weight[0], (1, 0, 2)).reshape(channels, -1)

    def lift(first, count):
        taps = jnp.stack(
            [
                raster_padded[:, first + dy : first + dy + count, :, dx : dx + cols]
                for dy in range(3)
                for dx in range(3)
            ],
            0,
        ).reshape((-1, count) + raster.shape[2:])
        return jnp.einsum("ok,krtw->rtow", lift_matrix, taps, preferred_element_type=jnp.float32)

    lifted = jnp.concatenate([lift(0, 1), lift(1, rows), lift(rows + 1, 1)], axis=0)
    coarse = jnp.transpose(padded_rows(coarse_features[0], "space", 1, 1), (1, 2, 0, 3))
    lifted = lifted + lift_bias[None, None, :, None] + coarse.astype(jnp.float32)
    line = lax.broadcasted_iota(jnp.int32, (rows + 2, 1, 1, 1), 0)
    inside = ((line > 0) | (space > 0)) & ((line < rows + 1) | (space < lax.axis_size("space") - 1))
    hidden_ext = jnp.where(inside, jnp.maximum(lifted, 0.0), 0.0).astype(jnp.bfloat16)

    split = (quarters, span) + hidden_ext.shape[1:]
    top = lax.slice_in_dim(hidden_ext, 0, rows, axis=0).reshape(split)
    bottom = lax.slice_in_dim(hidden_ext, 2, rows + 2, axis=0).reshape(split)
    windows = jnp.concatenate([top, lax.slice_in_dim(bottom, span - 2, span, axis=1)], axis=1)
    windows = jnp.transpose(windows, (2, 0, 1, 3, 4)).reshape((n, span + 2) + hidden_ext.shape[2:])
    gathered = lax.all_to_all(windows, "rot", 0, 0)

    spread = jnp.broadcast_to(group_weight, (n,) + group_weight.shape[1:])
    filters = lax.all_to_all(spread, "rot", 0, 0)
    bias = jnp.tile(group_bias, n)[:, None]
    mixed = group_mix(circulant_bank(filters), bias, gathered)

    returned = lax.all_to_all(mixed, "rot", 0, 0)
    returned = returned.reshape((tiles, quarters) + returned.shape[1:])
    result = jnp.transpose(returned, (3, 1, 2, 0, 4)).reshape((channels, rows, tiles, cols))
    return result[None]


def solution(mesh):
    return jax.shard_map(
        shards,
        mesh=mesh,
        in_specs=(
            P(None, "space", None, None),
            P("rot", None, "space", None, None),
            P("rot", None, None, None),
            P(),
            P("rot", None, None, None),
            P(),
        ),
        out_specs=P("rot", None, "space", None, None),
        check_vma=False,
    )
```

```python
import jax
import jax.numpy as jnp
from jax import lax
from jax.experimental import pallas as pl
from jax.experimental.pallas import tpu as pltpu
from jax.sharding import PartitionSpec as P


def padded_rows(array, axis, dim, width):
    size, length = lax.axis_size(axis), array.shape[dim]
    up = [(i, i + 1) for i in range(size - 1)]
    down = [(j, i) for i, j in up]
    last = lax.slice_in_dim(array, length - width, length, axis=dim)
    leading = lax.slice_in_dim(array, 0, width, axis=dim)
    before = lax.ppermute(last, axis, up)
    after = lax.ppermute(leading, axis, down)
    return jnp.concatenate([before, array, after], axis=dim)


def bank_kernel(pairs_ref, bank_ref):
    count, _, channels, lanes = pairs_ref.shape
    for g in range(count):
        for p in range(bank_ref.shape[2] // lanes):
            bank_ref[:, g * channels : (g + 1) * channels, p * lanes : (p + 1) * lanes] = pairs_ref[
                (g - 2 * p) % count
            ]


def circulant_bank(filters):
    count, taps, channels, _ = filters.shape
    pairs = jnp.concatenate([filters, jnp.roll(filters, 1, axis=0)], axis=-1)
    return pl.pallas_call(
        bank_kernel,
        out_shape=jax.ShapeDtypeStruct((taps, count * channels, count * channels), filters.dtype),
    )(pairs)


def mixing_kernel(bank_ref, bias_ref, x_ref, o_ref):
    row = pl.program_id(0)
    count, channels, cols = x_ref.shape[0], x_ref.shape[2], x_ref.shape[3]
    planes = [jnp.concatenate([x_ref[h, row + dy] for h in range(count)], axis=0) for dy in range(3)]
    sums = []
    for dx in range(3):
        total = None
        for dy in range(3):
            term = jnp.dot(bank_ref[3 * dy + dx], planes[dy], preferred_element_type=jnp.float32)
            total = term if total is None else total + term
        sums.append(total)
    column = lax.broadcasted_iota(jnp.int32, sums[0].shape, 1)
    left = jnp.where(column == 0, 0.0, pltpu.roll(sums[0], 1, 1))
    right = jnp.where(column == cols - 1, 0.0, pltpu.roll(sums[2], cols - 1, 1))
    mixed = sums[1] + left + right + bias_ref[...]
    mixed = jnp.maximum(mixed, 0.0).astype(o_ref.dtype)
    for g in range(count):
        o_ref[g, 0] = mixed[g * channels : (g + 1) * channels]


def group_mix(bank, bias, windows):
    count, rows_in, channels, cols = windows.shape
    rows_out = rows_in - 2
    full = count * channels
    return pl.pallas_call(
        mixing_kernel,
        grid=(rows_out,),
        in_specs=[
            pl.BlockSpec((9, full, full), lambda r: (0, 0, 0)),
            pl.BlockSpec((full, 1), lambda r: (0, 0)),
            pl.BlockSpec(windows.shape, lambda r: (0, 0, 0, 0)),
        ],
        out_specs=pl.BlockSpec((count, 1, channels, cols), lambda r: (0, r, 0, 0)),
        out_shape=jax.ShapeDtypeStruct((count, rows_out, channels, cols), jnp.bfloat16),
        compiler_params=pltpu.CompilerParams(vmem_limit_bytes=48 * 1024 * 1024),
    )(bank, bias, windows)


def shards(raster, coarse_features, lift_weight, lift_bias, group_weight, group_bias):
    n = lax.axis_size("rot")
    channels = lift_weight.shape[2]
    rows = raster.shape[1]
    chunk = rows // n

    tiles, cols = raster.shape[2], raster.shape[3]
    quarters = n // tiles
    span = rows // quarters
    space = lax.axis_index("space")

    raster_padded = jnp.pad(padded_rows(raster, "space", 1, 2), ((0, 0), (0, 0), (0, 0), (1, 1)))
    lift_matrix = jnp.transpose(lift_weight[0], (1, 0, 2)).reshape(channels, -1)

    def lift(first, count):
        taps = jnp.stack(
            [
                raster_padded[:, first + dy : first + dy + count, :, dx : dx + cols]
                for dy in range(3)
                for dx in range(3)
            ],
            0,
        ).reshape((-1, count) + raster.shape[2:])
        return jnp.einsum("ok,krtw->rtow", lift_matrix, taps, preferred_element_type=jnp.float32)

    lifted = jnp.concatenate([lift(0, 1), lift(1, rows), lift(rows + 1, 1)], axis=0)
    coarse = jnp.transpose(padded_rows(coarse_features[0], "space", 1, 1), (1, 2, 0, 3))
    lifted = lifted + lift_bias[None, None, :, None] + coarse.astype(jnp.float32)
    line = lax.broadcasted_iota(jnp.int32, (rows + 2, 1, 1, 1), 0)
    inside = ((line > 0) | (space > 0)) & ((line < rows + 1) | (space < lax.axis_size("space") - 1))
    hidden_ext = jnp.where(inside, jnp.maximum(lifted, 0.0), 0.0).astype(jnp.bfloat16)

    split = (quarters, span) + hidden_ext.shape[1:]
    top = lax.slice_in_dim(hidden_ext, 0, rows, axis=0).reshape(split)
    bottom = lax.slice_in_dim(hidden_ext, 2, rows + 2, axis=0).reshape(split)
    windows = jnp.concatenate([top, lax.slice_in_dim(bottom, span - 2, span, axis=1)], axis=1)
    windows = jnp.transpose(windows, (2, 0, 1, 3, 4)).reshape((n, span + 2) + hidden_ext.shape[2:])
    gathered = lax.all_to_all(windows, "rot", 0, 0)

    slots = jnp.zeros((n,) + group_weight.shape[1:], group_weight.dtype)
    slots = lax.dynamic_update_index_in_dim(slots, group_weight[0], lax.axis_index("rot"), 0)
    filters = lax.psum(slots, "rot")
    bias = jnp.tile(group_bias, n)[:, None]
    mixed = group_mix(circulant_bank(filters), bias, gathered)

    returned = lax.all_to_all(mixed, "rot", 0, 0)
    returned = returned.reshape((tiles, quarters) + returned.shape[1:])
    result = jnp.transpose(returned, (3, 1, 2, 0, 4)).reshape((channels, rows, tiles, cols))
    return result[None]


def solution(mesh):
    return jax.shard_map(
        shards,
        mesh=mesh,
        in_specs=(
            P(None, "space", None, None),
            P("rot", None, "space", None, None),
            P("rot", None, None, None),
            P(),
            P("rot", None, None, None),
            P(),
        ),
        out_specs=P("rot", None, "space", None, None),
        check_vma=False,
    )
```

```python
import jax
import jax.numpy as jnp
from jax import lax
from jax.experimental import pallas as pl
from jax.experimental.pallas import tpu as pltpu
from jax.sharding import PartitionSpec as P


def padded_rows(array, axis, dim, width):
    size, length = lax.axis_size(axis), array.shape[dim]
    up = [(i, i + 1) for i in range(size - 1)]
    down = [(j, i) for i, j in up]
    last = lax.slice_in_dim(array, length - width, length, axis=dim)
    leading = lax.slice_in_dim(array, 0, width, axis=dim)
    before = lax.ppermute(last, axis, up)
    after = lax.ppermute(leading, axis, down)
    return jnp.concatenate([before, array, after], axis=dim)


def bank_kernel(pairs_ref, bank_ref):
    count, _, channels, lanes = pairs_ref.shape
    for g in range(count):
        for p in range(bank_ref.shape[2] // lanes):
            bank_ref[:, g * channels : (g + 1) * channels, p * lanes : (p + 1) * lanes] = pairs_ref[
                (g - 2 * p) % count
            ]


def circulant_bank(filters):
    count, taps, channels, _ = filters.shape
    pairs = jnp.concatenate([filters, jnp.roll(filters, 1, axis=0)], axis=-1)
    return pl.pallas_call(
        bank_kernel,
        out_shape=jax.ShapeDtypeStruct((taps, count * channels, count * channels), filters.dtype),
    )(pairs)


def mixing_kernel(bank_ref, bias_ref, x_ref, o_ref):
    row = pl.program_id(0)
    count, channels, cols = x_ref.shape[0], x_ref.shape[2], x_ref.shape[3]
    planes = [jnp.concatenate([x_ref[h, row + dy] for h in range(count)], axis=0) for dy in range(3)]
    sums = []
    for dx in range(3):
        total = None
        for dy in range(3):
            term = jnp.dot(bank_ref[3 * dy + dx], planes[dy], preferred_element_type=jnp.float32)
            total = term if total is None else total + term
        sums.append(total)
    column = lax.broadcasted_iota(jnp.int32, sums[0].shape, 1)
    left = jnp.where(column == 0, 0.0, pltpu.roll(sums[0], 1, 1))
    right = jnp.where(column == cols - 1, 0.0, pltpu.roll(sums[2], cols - 1, 1))
    mixed = sums[1] + left + right + bias_ref[...]
    mixed = jnp.maximum(mixed, 0.0).astype(o_ref.dtype)
    for g in range(count):
        o_ref[g, 0] = mixed[g * channels : (g + 1) * channels]


def group_mix(bank, bias, windows):
    count, rows_in, channels, cols = windows.shape
    rows_out = rows_in - 2
    full = count * channels
    return pl.pallas_call(
        mixing_kernel,
        grid=(rows_out,),
        in_specs=[
            pl.BlockSpec((9, full, full), lambda r: (0, 0, 0)),
            pl.BlockSpec((full, 1), lambda r: (0, 0)),
            pl.BlockSpec(windows.shape, lambda r: (0, 0, 0, 0)),
        ],
        out_specs=pl.BlockSpec((count, 1, channels, cols), lambda r: (0, r, 0, 0)),
        out_shape=jax.ShapeDtypeStruct((count, rows_out, channels, cols), jnp.bfloat16),
        compiler_params=pltpu.CompilerParams(vmem_limit_bytes=48 * 1024 * 1024),
    )(bank, bias, windows)


def shards(raster, coarse_features, lift_weight, lift_bias, group_weight, group_bias):
    n = lax.axis_size("rot")
    channels = lift_weight.shape[2]
    rows = raster.shape[1]
    chunk = rows // n

    tiles, cols = raster.shape[2], raster.shape[3]
    quarters = n // tiles
    span = rows // quarters
    space = lax.axis_index("space")

    lift_matrix = jnp.transpose(lift_weight[0], (1, 0, 2)).reshape(channels, -1)
    size = lax.axis_size("space")
    above = lax.ppermute(raster[:, rows - 2 :], "space", [(i, i + 1) for i in range(size - 1)])
    below = lax.ppermute(raster[:, :2], "space", [(i + 1, i) for i in range(size - 1)])

    def lift(source):
        count = source.shape[1] - 2
        widened = jnp.transpose(jnp.pad(source, ((0, 0), (0, 0), (0, 0), (1, 1))), (1, 2, 0, 3))
        taps = jnp.concatenate(
            [widened[dy : dy + count, :, :, dx : dx + cols] for dy in range(3) for dx in range(3)], 2
        )
        return jnp.einsum("ok,rtkw->rtow", lift_matrix, taps, preferred_element_type=jnp.float32)

    body = jnp.concatenate([above[:, 1:], raster, below[:, :1]], axis=1)
    first = jnp.concatenate([above, raster[:, :1]], axis=1)
    last = jnp.concatenate([raster[:, rows - 1 :], below], axis=1)
    lifted = jnp.concatenate([lift(first), lift(body), lift(last)], axis=0)
    coarse = jnp.transpose(padded_rows(coarse_features[0], "space", 1, 1), (1, 2, 0, 3))
    lifted = lifted + lift_bias[None, None, :, None] + coarse.astype(jnp.float32)
    line = lax.broadcasted_iota(jnp.int32, (rows + 2, 1, 1, 1), 0)
    inside = ((line > 0) | (space > 0)) & ((line < rows + 1) | (space < lax.axis_size("space") - 1))
    hidden_ext = jnp.where(inside, jnp.maximum(lifted, 0.0), 0.0).astype(jnp.bfloat16)

    split = (quarters, span) + hidden_ext.shape[1:]
    top = lax.slice_in_dim(hidden_ext, 0, rows, axis=0).reshape(split)
    bottom = lax.slice_in_dim(hidden_ext, 2, rows + 2, axis=0).reshape(split)
    windows = jnp.concatenate([top, lax.slice_in_dim(bottom, span - 2, span, axis=1)], axis=1)
    windows = jnp.transpose(windows, (2, 0, 1, 3, 4)).reshape((n, span + 2) + hidden_ext.shape[2:])
    gathered = lax.all_to_all(windows, "rot", 0, 0)

    spread = jnp.broadcast_to(group_weight, (n,) + group_weight.shape[1:])
    filters = lax.all_to_all(spread, "rot", 0, 0)
    bias = jnp.tile(group_bias, n)[:, None]
    mixed = group_mix(circulant_bank(filters), bias, gathered)

    returned = lax.all_to_all(mixed, "rot", 0, 0)
    returned = returned.reshape((tiles, quarters) + returned.shape[1:])
    result = jnp.transpose(returned, (3, 1, 2, 0, 4)).reshape((channels, rows, tiles, cols))
    return result[None]


def solution(mesh):
    return jax.shard_map(
        shards,
        mesh=mesh,
        in_specs=(
            P(None, "space", None, None),
            P("rot", None, "space", None, None),
            P("rot", None, None, None),
            P(),
            P("rot", None, None, None),
            P(),
        ),
        out_specs=P("rot", None, "space", None, None),
        check_vma=False,
    )
```

```python
import jax
import jax.numpy as jnp
from jax import lax
from jax.experimental import pallas as pl
from jax.experimental.pallas import tpu as pltpu
from jax.sharding import PartitionSpec as P


def bank_kernel(pairs_ref, bank_ref):
    count, _, channels, lanes = pairs_ref.shape
    for g in range(count):
        for p in range(bank_ref.shape[2] // lanes):
            bank_ref[:, g * channels : (g + 1) * channels, p * lanes : (p + 1) * lanes] = pairs_ref[
                (g - 2 * p) % count
            ]


def circulant_bank(filters):
    count, taps, channels, _ = filters.shape
    pairs = jnp.concatenate([filters, jnp.roll(filters, 1, axis=0)], axis=-1)
    return pl.pallas_call(
        bank_kernel,
        out_shape=jax.ShapeDtypeStruct((taps, count * channels, count * channels), filters.dtype),
    )(pairs)


def mixing_kernel(bank_ref, bias_ref, x_ref, o_ref):
    row = pl.program_id(0)
    count, channels, cols = x_ref.shape[0], x_ref.shape[2], x_ref.shape[3]
    planes = [jnp.concatenate([x_ref[h, row + dy] for h in range(count)], axis=0) for dy in range(3)]
    sums = []
    for dx in range(3):
        total = None
        for dy in range(3):
            term = jnp.dot(bank_ref[3 * dy + dx], planes[dy], preferred_element_type=jnp.float32)
            total = term if total is None else total + term
        sums.append(total)
    column = lax.broadcasted_iota(jnp.int32, sums[0].shape, 1)
    left = jnp.where(column == 0, 0.0, pltpu.roll(sums[0], 1, 1))
    right = jnp.where(column == cols - 1, 0.0, pltpu.roll(sums[2], cols - 1, 1))
    mixed = sums[1] + left + right + bias_ref[...]
    mixed = jnp.maximum(mixed, 0.0).astype(o_ref.dtype)
    for g in range(count):
        o_ref[g, 0] = mixed[g * channels : (g + 1) * channels]


def group_mix(bank, bias, windows):
    count, rows_in, channels, cols = windows.shape
    rows_out = rows_in - 2
    full = count * channels
    return pl.pallas_call(
        mixing_kernel,
        grid=(rows_out,),
        in_specs=[
            pl.BlockSpec((9, full, full), lambda r: (0, 0, 0)),
            pl.BlockSpec((full, 1), lambda r: (0, 0)),
            pl.BlockSpec(windows.shape, lambda r: (0, 0, 0, 0)),
        ],
        out_specs=pl.BlockSpec((count, 1, channels, cols), lambda r: (0, r, 0, 0)),
        out_shape=jax.ShapeDtypeStruct((count, rows_out, channels, cols), jnp.bfloat16),
        compiler_params=pltpu.CompilerParams(vmem_limit_bytes=48 * 1024 * 1024),
    )(bank, bias, windows)


def layer(raster, coarse_features, lift_weight, lift_bias, group_weight, group_bias):
    n = lax.axis_size("rot")
    channels = lift_weight.shape[2]
    rows = raster.shape[1]

    tiles, cols = raster.shape[2], raster.shape[3]
    quarters = n // tiles
    span = rows // quarters
    space = lax.axis_index("space")

    lift_matrix = jnp.transpose(lift_weight[0], (1, 0, 2)).reshape(channels, -1)
    size = lax.axis_size("space")
    coarse_own = coarse_features[0]
    halo_shape = (-1,) + raster.shape[2:]

    def edges(raster_rows, coarse_row):
        return jnp.concatenate([raster_rows.reshape(halo_shape), coarse_row.reshape(halo_shape)], 0)

    up = [(i, i + 1) for i in range(size - 1)]
    from_above = lax.ppermute(edges(raster[:, rows - 2 :], coarse_own[:, rows - 1]), "space", up)
    from_below = lax.ppermute(edges(raster[:, :2], coarse_own[:, 0]), "space", [(j, i) for i, j in up])
    split_at = 2 * raster.shape[0]
    above = from_above[:split_at].reshape((-1, 2) + raster.shape[2:])
    below = from_below[:split_at].reshape((-1, 2) + raster.shape[2:])
    coarse_ext = jnp.concatenate(
        [from_above[split_at:][:, None], coarse_own, from_below[split_at:][:, None]], axis=1
    )

    def lift(source):
        count = source.shape[1] - 2
        widened = jnp.transpose(jnp.pad(source, ((0, 0), (0, 0), (0, 0), (1, 1))), (1, 2, 0, 3))
        taps = jnp.concatenate(
            [widened[dy : dy + count, :, :, dx : dx + cols] for dy in range(3) for dx in range(3)], 2
        )
        return jnp.einsum("ok,rtkw->rtow", lift_matrix, taps, preferred_element_type=jnp.float32)

    body = jnp.concatenate([above[:, 1:], raster, below[:, :1]], axis=1)
    first = jnp.concatenate([above, raster[:, :1]], axis=1)
    last = jnp.concatenate([raster[:, rows - 1 :], below], axis=1)
    lifted = jnp.concatenate([lift(first), lift(body), lift(last)], axis=0)
    coarse = jnp.transpose(coarse_ext, (1, 2, 0, 3))
    lifted = lifted + lift_bias[None, None, :, None] + coarse.astype(jnp.float32)
    line = lax.broadcasted_iota(jnp.int32, (rows + 2, 1, 1, 1), 0)
    inside = ((line > 0) | (space > 0)) & ((line < rows + 1) | (space < lax.axis_size("space") - 1))
    hidden_ext = jnp.where(inside, jnp.maximum(lifted, 0.0), 0.0).astype(jnp.bfloat16)

    split = (quarters, span) + hidden_ext.shape[1:]
    top = lax.slice_in_dim(hidden_ext, 0, rows, axis=0).reshape(split)
    bottom = lax.slice_in_dim(hidden_ext, 2, rows + 2, axis=0).reshape(split)
    windows = jnp.concatenate([top, lax.slice_in_dim(bottom, span - 2, span, axis=1)], axis=1)
    windows = jnp.transpose(windows, (2, 0, 1, 3, 4)).reshape((n, span + 2) + hidden_ext.shape[2:])
    gathered = lax.all_to_all(windows, "rot", 0, 0)

    came = [group_weight[0]] + [
        lax.ppermute(group_weight[0], "rot", [(i, (i + d) % n) for i in range(n)]) for d in range(1, n)
    ]
    filters = jnp.roll(jnp.stack([came[(-j) % n] for j in range(n)]), lax.axis_index("rot"), axis=0)
    bias = jnp.tile(group_bias, n)[:, None]
    mixed = group_mix(circulant_bank(filters), bias, gathered)

    returned = lax.all_to_all(mixed, "rot", 0, 0)
    returned = returned.reshape((tiles, quarters) + returned.shape[1:])
    result = jnp.transpose(returned, (3, 1, 2, 0, 4)).reshape((channels, rows, tiles, cols))
    return result[None]


def solution(mesh):
    return jax.shard_map(
        layer,
        mesh=mesh,
        in_specs=(
            P(None, "space", None, None),
            P("rot", None, "space", None, None),
            P("rot", None, None, None),
            P(),
            P("rot", None, None, None),
            P(),
        ),
        out_specs=P("rot", None, "space", None, None),
        check_vma=False,
    )
```

```python
import jax
import jax.numpy as jnp
from jax import lax
from jax.experimental import pallas as pl
from jax.experimental.pallas import tpu as pltpu
from jax.sharding import PartitionSpec as P


def bank_kernel(pairs_ref, bank_ref):
    count, _, channels, lanes = pairs_ref.shape
    for g in range(count):
        for p in range(bank_ref.shape[2] // lanes):
            bank_ref[:, g * channels : (g + 1) * channels, p * lanes : (p + 1) * lanes] = pairs_ref[
                (g - 2 * p) % count
            ]


def circulant_bank(filters):
    count, taps, channels, _ = filters.shape
    pairs = jnp.concatenate([filters, jnp.roll(filters, 1, axis=0)], axis=-1)
    return pl.pallas_call(
        bank_kernel,
        out_shape=jax.ShapeDtypeStruct((taps, count * channels, count * channels), filters.dtype),
    )(pairs)


def mixing_kernel(bank_ref, bias_ref, x_ref, o_ref):
    row = pl.program_id(0)
    count, channels, cols = x_ref.shape[0], x_ref.shape[2], x_ref.shape[3]
    planes = [jnp.concatenate([x_ref[h, row + dy] for h in range(count)], axis=0) for dy in range(3)]
    sums = []
    for dx in range(3):
        total = None
        for dy in range(3):
            term = jnp.dot(bank_ref[3 * dy + dx], planes[dy], preferred_element_type=jnp.float32)
            total = term if total is None else total + term
        sums.append(total)
    column = lax.broadcasted_iota(jnp.int32, sums[0].shape, 1)
    left = jnp.where(column == 0, 0.0, pltpu.roll(sums[0], 1, 1))
    right = jnp.where(column == cols - 1, 0.0, pltpu.roll(sums[2], cols - 1, 1))
    mixed = sums[1] + left + right + bias_ref[...]
    mixed = jnp.maximum(mixed, 0.0).astype(o_ref.dtype)
    for g in range(count):
        o_ref[g, 0] = mixed[g * channels : (g + 1) * channels]


def group_mix(bank, bias, windows):
    count, rows_in, channels, cols = windows.shape
    rows_out = rows_in - 2
    full = count * channels
    return pl.pallas_call(
        mixing_kernel,
        grid=(rows_out,),
        in_specs=[
            pl.BlockSpec((9, full, full), lambda r: (0, 0, 0)),
            pl.BlockSpec((full, 1), lambda r: (0, 0)),
            pl.BlockSpec(windows.shape, lambda r: (0, 0, 0, 0)),
        ],
        out_specs=pl.BlockSpec((count, 1, channels, cols), lambda r: (0, r, 0, 0)),
        out_shape=jax.ShapeDtypeStruct((count, rows_out, channels, cols), jnp.bfloat16),
        compiler_params=pltpu.CompilerParams(vmem_limit_bytes=48 * 1024 * 1024),
    )(bank, bias, windows)


def shards(raster, coarse_features, lift_weight, lift_bias, group_weight, group_bias):
    n = lax.axis_size("rot")
    channels = lift_weight.shape[2]
    rows = raster.shape[1]
    chunk = rows // n

    tiles, cols = raster.shape[2], raster.shape[3]
    quarters = n // tiles
    span = rows // quarters
    space = lax.axis_index("space")

    lift_matrix = jnp.transpose(lift_weight[0], (1, 0, 2)).reshape(channels, -1)
    size = lax.axis_size("space")
    coarse_own = coarse_features[0]
    halo_shape = (-1,) + raster.shape[2:]

    def edges(raster_rows, coarse_row):
        return jnp.concatenate([raster_rows.reshape(halo_shape), coarse_row.reshape(halo_shape)], 0)

    up = [(i, i + 1) for i in range(size - 1)]
    from_above = lax.ppermute(edges(raster[:, rows - 2 :], coarse_own[:, rows - 1]), "space", up)
    from_below = lax.ppermute(edges(raster[:, :2], coarse_own[:, 0]), "space", [(j, i) for i, j in up])
    split_at = 2 * raster.shape[0]
    above = from_above[:split_at].reshape((-1, 2) + raster.shape[2:])
    below = from_below[:split_at].reshape((-1, 2) + raster.shape[2:])
    coarse_ext = jnp.concatenate(
        [from_above[split_at:][:, None], coarse_own, from_below[split_at:][:, None]], axis=1
    )

    def lift(source):
        count = source.shape[1] - 2
        widened = jnp.transpose(jnp.pad(source, ((0, 0), (0, 0), (0, 0), (1, 1))), (1, 2, 0, 3))
        taps = jnp.concatenate(
            [widened[dy : dy + count, :, :, dx : dx + cols] for dy in range(3) for dx in range(3)], 2
        )
        return jnp.einsum("ok,rtkw->rtow", lift_matrix, taps, preferred_element_type=jnp.float32)

    body = jnp.concatenate([above[:, 1:], raster, below[:, :1]], axis=1)
    first = jnp.concatenate([above, raster[:, :1]], axis=1)
    last = jnp.concatenate([raster[:, rows - 1 :], below], axis=1)
    lifted = jnp.concatenate([lift(first), lift(body), lift(last)], axis=0)
    coarse = jnp.transpose(coarse_ext, (1, 2, 0, 3))
    lifted = lifted + lift_bias[None, None, :, None] + coarse.astype(jnp.float32)
    line = lax.broadcasted_iota(jnp.int32, (rows + 2, 1, 1, 1), 0)
    inside = ((line > 0) | (space > 0)) & ((line < rows + 1) | (space < lax.axis_size("space") - 1))
    hidden_ext = jnp.where(inside, jnp.maximum(lifted, 0.0), 0.0).astype(jnp.bfloat16)

    split = (quarters, span) + hidden_ext.shape[1:]
    top = lax.slice_in_dim(hidden_ext, 0, rows, axis=0).reshape(split)
    bottom = lax.slice_in_dim(hidden_ext, 2, rows + 2, axis=0).reshape(split)
    windows = jnp.concatenate([top, lax.slice_in_dim(bottom, span - 2, span, axis=1)], axis=1)
    windows = jnp.transpose(windows, (2, 0, 1, 3, 4)).reshape((n, span + 2) + hidden_ext.shape[2:])
    gathered = lax.all_to_all(windows, "rot", 0, 0)

    spread = jnp.broadcast_to(group_weight, (n,) + group_weight.shape[1:])
    filters = lax.all_to_all(spread, "rot", 0, 0)
    bias = jnp.tile(group_bias, n)[:, None]
    mixed = group_mix(circulant_bank(filters), bias, gathered)

    returned = lax.all_to_all(mixed, "rot", 0, 0)
    returned = returned.reshape((tiles, quarters) + returned.shape[1:])
    result = jnp.transpose(returned, (3, 1, 2, 0, 4)).reshape((channels, rows, tiles, cols))
    return result[None]


def solution(mesh):
    return jax.shard_map(
        shards,
        mesh=mesh,
        in_specs=(
            P(None, "space", None, None),
            P("rot", None, "space", None, None),
            P("rot", None, None, None),
            P(),
            P("rot", None, None, None),
            P(),
        ),
        out_specs=P("rot", None, "space", None, None),
        check_vma=False,
    )
```

```python
import jax
import jax.numpy as jnp
from jax import lax
from jax.experimental import pallas as pl
from jax.experimental.pallas import tpu as pltpu
from jax.sharding import PartitionSpec as P


def bank_kernel(pairs_ref, bank_ref):
    count, _, channels, lanes = pairs_ref.shape
    for g in range(count):
        for p in range(bank_ref.shape[2] // lanes):
            bank_ref[:, g * channels : (g + 1) * channels, p * lanes : (p + 1) * lanes] = pairs_ref[
                (g - 2 * p) % count
            ]


def circulant_bank(filters):
    count, taps, channels, _ = filters.shape
    pairs = jnp.concatenate([filters, jnp.roll(filters, 1, axis=0)], axis=-1)
    return pl.pallas_call(
        bank_kernel,
        out_shape=jax.ShapeDtypeStruct((taps, count * channels, count * channels), filters.dtype),
    )(pairs)


def mixing_kernel(bank_ref, bias_ref, x_ref, o_ref):
    row = pl.program_id(0)
    count, channels, cols = o_ref.shape[0], o_ref.shape[2], o_ref.shape[3]
    planes = [x_ref[row + dy] for dy in range(3)]
    sums = []
    for dx in range(3):
        total = None
        for dy in range(3):
            term = jnp.dot(bank_ref[3 * dy + dx], planes[dy], preferred_element_type=jnp.float32)
            total = term if total is None else total + term
        sums.append(total)
    column = lax.broadcasted_iota(jnp.int32, sums[0].shape, 1)
    left = jnp.where(column == 0, 0.0, pltpu.roll(sums[0], 1, 1))
    right = jnp.where(column == cols - 1, 0.0, pltpu.roll(sums[2], cols - 1, 1))
    mixed = sums[1] + left + right + bias_ref[...]
    mixed = jnp.maximum(mixed, 0.0).astype(o_ref.dtype)
    for g in range(count):
        o_ref[g, 0] = mixed[g * channels : (g + 1) * channels]


def group_mix(bank, bias, windows, count):
    rows_in, full, cols = windows.shape
    channels = full // count
    rows_out = rows_in - 2
    return pl.pallas_call(
        mixing_kernel,
        grid=(rows_out,),
        in_specs=[
            pl.BlockSpec((9, full, full), lambda r: (0, 0, 0)),
            pl.BlockSpec((full, 1), lambda r: (0, 0)),
            pl.BlockSpec(windows.shape, lambda r: (0, 0, 0)),
        ],
        out_specs=pl.BlockSpec((count, 1, channels, cols), lambda r: (0, r, 0, 0)),
        out_shape=jax.ShapeDtypeStruct((count, rows_out, channels, cols), jnp.bfloat16),
        compiler_params=pltpu.CompilerParams(vmem_limit_bytes=48 * 1024 * 1024),
    )(bank, bias, windows)


def shards(raster, coarse_features, lift_weight, lift_bias, group_weight, group_bias):
    n = lax.axis_size("rot")
    channels = lift_weight.shape[2]
    rows = raster.shape[1]
    chunk = rows // n

    tiles, cols = raster.shape[2], raster.shape[3]
    quarters = n // tiles
    span = rows // quarters
    space = lax.axis_index("space")

    lift_matrix = jnp.transpose(lift_weight[0], (1, 0, 2)).reshape(channels, -1)
    size = lax.axis_size("space")
    coarse_own = coarse_features[0]
    halo_shape = (-1,) + raster.shape[2:]

    def edges(raster_rows, coarse_row):
        return jnp.concatenate([raster_rows.reshape(halo_shape), coarse_row.reshape(halo_shape)], 0)

    up = [(i, i + 1) for i in range(size - 1)]
    from_above = lax.ppermute(edges(raster[:, rows - 2 :], coarse_own[:, rows - 1]), "space", up)
    from_below = lax.ppermute(edges(raster[:, :2], coarse_own[:, 0]), "space", [(j, i) for i, j in up])
    split_at = 2 * raster.shape[0]
    above = from_above[:split_at].reshape((-1, 2) + raster.shape[2:])
    below = from_below[:split_at].reshape((-1, 2) + raster.shape[2:])
    coarse_ext = jnp.concatenate(
        [from_above[split_at:][:, None], coarse_own, from_below[split_at:][:, None]], axis=1
    )

    def lift(source):
        count = source.shape[1] - 2
        widened = jnp.transpose(jnp.pad(source, ((0, 0), (0, 0), (0, 0), (1, 1))), (1, 2, 0, 3))
        taps = jnp.concatenate(
            [widened[dy : dy + count, :, :, dx : dx + cols] for dy in range(3) for dx in range(3)], 2
        )
        return jnp.einsum("ok,rtkw->rtow", lift_matrix, taps, preferred_element_type=jnp.float32)

    body = jnp.concatenate([above[:, 1:], raster, below[:, :1]], axis=1)
    first = jnp.concatenate([above, raster[:, :1]], axis=1)
    last = jnp.concatenate([raster[:, rows - 1 :], below], axis=1)
    lifted = jnp.concatenate([lift(first), lift(body), lift(last)], axis=0)
    coarse = jnp.transpose(coarse_ext, (1, 2, 0, 3))
    lifted = lifted + lift_bias[None, None, :, None] + coarse.astype(jnp.float32)
    line = lax.broadcasted_iota(jnp.int32, (rows + 2, 1, 1, 1), 0)
    inside = ((line > 0) | (space > 0)) & ((line < rows + 1) | (space < lax.axis_size("space") - 1))
    hidden_ext = jnp.where(inside, jnp.maximum(lifted, 0.0), 0.0).astype(jnp.bfloat16)

    split = (quarters, span) + hidden_ext.shape[1:]
    top = lax.slice_in_dim(hidden_ext, 0, rows, axis=0).reshape(split)
    bottom = lax.slice_in_dim(hidden_ext, 2, rows + 2, axis=0).reshape(split)
    windows = jnp.concatenate([top, lax.slice_in_dim(bottom, span - 2, span, axis=1)], axis=1)
    windows = jnp.transpose(windows, (2, 0, 1, 3, 4)).reshape((n, span + 2) + hidden_ext.shape[2:])
    gathered = lax.all_to_all(windows, "rot", 0, 1)
    gathered = gathered.reshape((gathered.shape[0], n * channels, cols))

    dense = group_weight[0].reshape(2, -1)
    spread = jnp.broadcast_to(dense, (n,) + dense.shape)
    filters = lax.all_to_all(spread, "rot", 0, 0).reshape((n,) + group_weight.shape[1:])
    bias = jnp.tile(group_bias, n)[:, None]
    mixed = group_mix(circulant_bank(filters), bias, gathered, n)

    returned = lax.all_to_all(mixed, "rot", 0, 0)
    returned = returned.reshape((tiles, quarters) + returned.shape[1:])
    result = jnp.transpose(returned, (3, 1, 2, 0, 4)).reshape((channels, rows, tiles, cols))
    return result[None]


def solution(mesh):
    return jax.shard_map(
        shards,
        mesh=mesh,
        in_specs=(
            P(None, "space", None, None),
            P("rot", None, "space", None, None),
            P("rot", None, None, None),
            P(),
            P("rot", None, None, None),
            P(),
        ),
        out_specs=P("rot", None, "space", None, None),
        check_vma=False,
    )
```

```python
import jax
import jax.numpy as jnp
from jax import lax
from jax.experimental import pallas as pl
from jax.experimental.pallas import tpu as pltpu
from jax.sharding import PartitionSpec as P


def bank_kernel(pairs_ref, bank_ref):
    count, _, channels, lanes = pairs_ref.shape
    for g in range(count):
        for p in range(bank_ref.shape[2] // lanes):
            bank_ref[:, g * channels : (g + 1) * channels, p * lanes : (p + 1) * lanes] = pairs_ref[
                (g - 2 * p) % count
            ]


def circulant_bank(filters):
    count, taps, channels, _ = filters.shape
    pairs = jnp.concatenate([filters, jnp.roll(filters, 1, axis=0)], axis=-1)
    return pl.pallas_call(
        bank_kernel,
        out_shape=jax.ShapeDtypeStruct((taps, count * channels, count * channels), filters.dtype),
    )(pairs)


def mixing_kernel(bank_ref, bias_ref, x_ref, o_ref):
    row = pl.program_id(0)
    count, channels, cols = o_ref.shape[0], o_ref.shape[2], o_ref.shape[3]
    planes = [x_ref[row + dy] for dy in range(3)]
    sums = []
    for dx in range(3):
        total = None
        for dy in range(3):
            term = jnp.dot(bank_ref[3 * dy + dx], planes[dy], preferred_element_type=jnp.float32)
            total = term if total is None else total + term
        sums.append(total)
    column = lax.broadcasted_iota(jnp.int32, sums[0].shape, 1)
    left = jnp.where(column == 0, 0.0, pltpu.roll(sums[0], 1, 1))
    right = jnp.where(column == cols - 1, 0.0, pltpu.roll(sums[2], cols - 1, 1))
    mixed = sums[1] + left + right + bias_ref[...]
    mixed = jnp.maximum(mixed, 0.0).astype(o_ref.dtype)
    for g in range(count):
        o_ref[g, 0] = mixed[g * channels : (g + 1) * channels]


def group_mix(bank, bias, windows, count):
    rows_in, full, cols = windows.shape
    channels = full // count
    rows_out = rows_in - 2
    return pl.pallas_call(
        mixing_kernel,
        grid=(rows_out,),
        in_specs=[
            pl.BlockSpec((9, full, full), lambda r: (0, 0, 0)),
            pl.BlockSpec((full, 1), lambda r: (0, 0)),
            pl.BlockSpec(windows.shape, lambda r: (0, 0, 0)),
        ],
        out_specs=pl.BlockSpec((count, 1, channels, cols), lambda r: (0, r, 0, 0)),
        out_shape=jax.ShapeDtypeStruct((count, rows_out, channels, cols), jnp.bfloat16),
        compiler_params=pltpu.CompilerParams(vmem_limit_bytes=48 * 1024 * 1024),
    )(bank, bias, windows)


def layer(raster, coarse_features, lift_weight, lift_bias, group_weight, group_bias):
    n = lax.axis_size("rot")
    channels = lift_weight.shape[2]
    rows = raster.shape[1]

    tiles, cols = raster.shape[2], raster.shape[3]
    quarters = n // tiles
    span = rows // quarters
    space = lax.axis_index("space")

    lift_matrix = jnp.transpose(lift_weight[0], (1, 0, 2)).reshape(channels, -1)
    size = lax.axis_size("space")
    coarse_own = coarse_features[0]
    halo_shape = (-1,) + raster.shape[2:]

    def edges(raster_rows, coarse_row):
        return jnp.concatenate([raster_rows.reshape(halo_shape), coarse_row.reshape(halo_shape)], 0)

    up = [(i, i + 1) for i in range(size - 1)]
    from_above = lax.ppermute(edges(raster[:, rows - 2 :], coarse_own[:, rows - 1]), "space", up)
    from_below = lax.ppermute(edges(raster[:, :2], coarse_own[:, 0]), "space", [(j, i) for i, j in up])
    split_at = 2 * raster.shape[0]
    above = from_above[:split_at].reshape((-1, 2) + raster.shape[2:])
    below = from_below[:split_at].reshape((-1, 2) + raster.shape[2:])
    coarse_ext = jnp.concatenate(
        [from_above[split_at:][:, None], coarse_own, from_below[split_at:][:, None]], axis=1
    )

    def lift(source):
        count = source.shape[1] - 2
        widened = jnp.transpose(jnp.pad(source, ((0, 0), (0, 0), (0, 0), (1, 1))), (1, 2, 0, 3))
        taps = jnp.concatenate(
            [widened[dy : dy + count, :, :, dx : dx + cols] for dy in range(3) for dx in range(3)], 2
        )
        return jnp.einsum("ok,rtkw->rtow", lift_matrix, taps, preferred_element_type=jnp.float32)

    body = jnp.concatenate([above[:, 1:], raster, below[:, :1]], axis=1)
    first = jnp.concatenate([above, raster[:, :1]], axis=1)
    last = jnp.concatenate([raster[:, rows - 1 :], below], axis=1)
    lifted = jnp.concatenate([lift(first), lift(body), lift(last)], axis=0)
    coarse = jnp.transpose(coarse_ext, (1, 2, 0, 3))
    lifted = lifted + lift_bias[None, None, :, None] + coarse.astype(jnp.float32)
    line = lax.broadcasted_iota(jnp.int32, (rows + 2, 1, 1, 1), 0)
    inside = ((line > 0) | (space > 0)) & ((line < rows + 1) | (space < lax.axis_size("space") - 1))
    hidden_ext = jnp.where(inside, jnp.maximum(lifted, 0.0), 0.0).astype(jnp.bfloat16)

    split = (quarters, span) + hidden_ext.shape[1:]
    top = lax.slice_in_dim(hidden_ext, 0, rows, axis=0).reshape(split)
    bottom = lax.slice_in_dim(hidden_ext, 2, rows + 2, axis=0).reshape(split)
    windows = jnp.concatenate([top, lax.slice_in_dim(bottom, span - 2, span, axis=1)], axis=1)
    windows = jnp.transpose(windows, (2, 0, 1, 3, 4)).reshape((n, span + 2) + hidden_ext.shape[2:])
    gathered = lax.all_to_all(windows, "rot", 0, 1)
    gathered = gathered.reshape((gathered.shape[0], n * channels, cols))

    dense = group_weight[0].reshape(2, -1)
    spread = jnp.broadcast_to(dense, (n,) + dense.shape)
    filters = lax.all_to_all(spread, "rot", 0, 0)
    filters = filters.reshape((n,) + group_weight.shape[1:])
    bias = jnp.tile(group_bias, n)[:, None]
    mixed = group_mix(circulant_bank(filters), bias, gathered, n)

    returned = lax.all_to_all(mixed, "rot", 0, 0)
    returned = returned.reshape((tiles, quarters) + returned.shape[1:])
    result = jnp.transpose(returned, (3, 1, 2, 0, 4)).reshape((channels, rows, tiles, cols))
    return result[None]


def solution(mesh):
    return jax.shard_map(
        layer,
        mesh=mesh,
        in_specs=(
            P(None, "space", None, None),
            P("rot", None, "space", None, None),
            P("rot", None, None, None),
            P(),
            P("rot", None, None, None),
            P(),
        ),
        out_specs=P("rot", None, "space", None, None),
        check_vma=False,
    )
```

```python
import jax
import jax.numpy as jnp
from jax import lax
from jax.experimental import pallas as pl
from jax.experimental.pallas import tpu as pltpu
from jax.sharding import PartitionSpec as P


def bank_kernel(pairs_ref, bank_ref):
    count, _, channels, lanes = pairs_ref.shape
    for g in range(count):
        for p in range(bank_ref.shape[2] // lanes):
            bank_ref[:, g * channels : (g + 1) * channels, p * lanes : (p + 1) * lanes] = pairs_ref[
                (g - 2 * p) % count
            ]


def circulant_bank(filters):
    count, taps, channels, _ = filters.shape
    pairs = jnp.concatenate([filters, jnp.roll(filters, 1, axis=0)], axis=-1)
    return pl.pallas_call(
        bank_kernel,
        out_shape=jax.ShapeDtypeStruct((taps, count * channels, count * channels), filters.dtype),
    )(pairs)


def mixing_kernel(bank_ref, bias_ref, x_ref, o_ref, acc_ref):
    dx, row = pl.program_id(0), pl.program_id(1)
    count, channels, cols = o_ref.shape[0], o_ref.shape[2], o_ref.shape[3]
    total = None
    for dy in range(3):
        term = jnp.dot(bank_ref[dy, 0], x_ref[row + dy], preferred_element_type=jnp.float32)
        total = term if total is None else total + term
    column = lax.broadcasted_iota(jnp.int32, total.shape, 1)

    @pl.when(dx == 0)
    def _():
        acc_ref[row] = jnp.where(column == 0, 0.0, pltpu.roll(total, 1, 1))

    @pl.when(dx == 1)
    def _():
        acc_ref[row] += total

    @pl.when(dx == 2)
    def _():
        right = jnp.where(column == cols - 1, 0.0, pltpu.roll(total, cols - 1, 1))
        mixed = jnp.maximum(acc_ref[row] + right + bias_ref[...], 0.0).astype(o_ref.dtype)
        for g in range(count):
            o_ref[g, 0] = mixed[g * channels : (g + 1) * channels]


def group_mix(bank, bias, windows, count):
    rows_in, full, cols = windows.shape
    channels = full // count
    rows_out = rows_in - 2
    return pl.pallas_call(
        mixing_kernel,
        grid=(3, rows_out),
        in_specs=[
            pl.BlockSpec((3, 1, full, full), lambda dx, r: (0, dx, 0, 0)),
            pl.BlockSpec((full, 1), lambda dx, r: (0, 0)),
            pl.BlockSpec(windows.shape, lambda dx, r: (0, 0, 0)),
        ],
        out_specs=pl.BlockSpec((count, 1, channels, cols), lambda dx, r: (0, jnp.where(dx == 2, r, 0), 0, 0)),
        out_shape=jax.ShapeDtypeStruct((count, rows_out, channels, cols), jnp.bfloat16),
        scratch_shapes=[pltpu.VMEM((rows_out, full, cols), jnp.float32)],
        compiler_params=pltpu.CompilerParams(vmem_limit_bytes=48 * 1024 * 1024),
    )(bank.reshape(3, 3, full, full), bias, windows)


def layer(raster, coarse_features, lift_weight, lift_bias, group_weight, group_bias):
    n = lax.axis_size("rot")
    channels = lift_weight.shape[2]
    rows = raster.shape[1]

    tiles, cols = raster.shape[2], raster.shape[3]
    quarters = n // tiles
    span = rows // quarters
    space = lax.axis_index("space")

    lift_matrix = jnp.transpose(lift_weight[0], (1, 0, 2)).reshape(channels, -1)
    size = lax.axis_size("space")
    coarse_own = coarse_features[0]
    halo_shape = (-1,) + raster.shape[2:]

    def edges(raster_rows, coarse_row):
        return jnp.concatenate([raster_rows.reshape(halo_shape), coarse_row.reshape(halo_shape)], 0)

    up = [(i, i + 1) for i in range(size - 1)]
    from_above = lax.ppermute(edges(raster[:, rows - 2 :], coarse_own[:, rows - 1]), "space", up)
    from_below = lax.ppermute(edges(raster[:, :2], coarse_own[:, 0]), "space", [(j, i) for i, j in up])
    split_at = 2 * raster.shape[0]
    above = from_above[:split_at].reshape((-1, 2) + raster.shape[2:])
    below = from_below[:split_at].reshape((-1, 2) + raster.shape[2:])
    coarse_ext = jnp.concatenate(
        [from_above[split_at:][:, None], coarse_own, from_below[split_at:][:, None]], axis=1
    )

    def lift(source):
        count = source.shape[1] - 2
        widened = jnp.transpose(jnp.pad(source, ((0, 0), (0, 0), (0, 0), (1, 1))), (1, 2, 0, 3))
        taps = jnp.concatenate(
            [widened[dy : dy + count, :, :, dx : dx + cols] for dy in range(3) for dx in range(3)], 2
        )
        return jnp.einsum("ok,rtkw->rtow", lift_matrix, taps, preferred_element_type=jnp.float32)

    body = jnp.concatenate([above[:, 1:], raster, below[:, :1]], axis=1)
    first = jnp.concatenate([above, raster[:, :1]], axis=1)
    last = jnp.concatenate([raster[:, rows - 1 :], below], axis=1)
    lifted = jnp.concatenate([lift(first), lift(body), lift(last)], axis=0)
    coarse = jnp.transpose(coarse_ext, (1, 2, 0, 3))
    lifted = lifted + lift_bias[None, None, :, None] + coarse.astype(jnp.float32)
    line = lax.broadcasted_iota(jnp.int32, (rows + 2, 1, 1, 1), 0)
    inside = ((line > 0) | (space > 0)) & ((line < rows + 1) | (space < lax.axis_size("space") - 1))
    hidden_ext = jnp.where(inside, jnp.maximum(lifted, 0.0), 0.0).astype(jnp.bfloat16)

    split = (quarters, span) + hidden_ext.shape[1:]
    top = lax.slice_in_dim(hidden_ext, 0, rows, axis=0).reshape(split)
    bottom = lax.slice_in_dim(hidden_ext, 2, rows + 2, axis=0).reshape(split)
    windows = jnp.concatenate([top, lax.slice_in_dim(bottom, span - 2, span, axis=1)], axis=1)
    windows = jnp.transpose(windows, (2, 0, 1, 3, 4)).reshape((n, span + 2) + hidden_ext.shape[2:])
    gathered = lax.all_to_all(windows, "rot", 0, 1)
    gathered = gathered.reshape((gathered.shape[0], n * channels, cols))

    dense = group_weight[0].reshape(2, -1)
    spread = jnp.broadcast_to(dense, (n,) + dense.shape)
    filters = lax.all_to_all(spread, "rot", 0, 0)
    filters = filters.reshape((n,) + group_weight.shape[1:])
    bias = jnp.tile(group_bias, n)[:, None]
    mixed = group_mix(circulant_bank(filters), bias, gathered, n)

    returned = lax.all_to_all(mixed, "rot", 0, 0)
    returned = returned.reshape((tiles, quarters) + returned.shape[1:])
    result = jnp.transpose(returned, (3, 1, 2, 0, 4)).reshape((channels, rows, tiles, cols))
    return result[None]


def solution(mesh):
    return jax.shard_map(
        layer,
        mesh=mesh,
        in_specs=(
            P(None, "space", None, None),
            P("rot", None, "space", None, None),
            P("rot", None, None, None),
            P(),
            P("rot", None, None, None),
            P(),
        ),
        out_specs=P("rot", None, "space", None, None),
        check_vma=False,
    )
```

```python
import jax
import jax.numpy as jnp
from jax import lax
from jax.experimental import pallas as pl
from jax.experimental.pallas import tpu as pltpu
from jax.sharding import PartitionSpec as P


def bank_kernel(pairs_ref, bank_ref):
    count, _, channels, lanes = pairs_ref.shape
    for g in range(count):
        for p in range(bank_ref.shape[2] // lanes):
            bank_ref[:, g * channels : (g + 1) * channels, p * lanes : (p + 1) * lanes] = pairs_ref[
                (g - 2 * p) % count
            ]


def circulant_bank(filters):
    count, taps, channels, _ = filters.shape
    pairs = jnp.concatenate([filters, jnp.roll(filters, 1, axis=0)], axis=-1)
    return pl.pallas_call(
        bank_kernel,
        out_shape=jax.ShapeDtypeStruct((taps, count * channels, count * channels), filters.dtype),
    )(pairs)


def mixing_kernel(bank_ref, bias_ref, x_ref, o_ref):
    count, rows_out, channels, cols = o_ref.shape
    width = rows_out * cols
    planes = [x_ref[:, dy * cols : dy * cols + width] for dy in range(3)]
    sums = []
    for dx in range(3):
        total = None
        for dy in range(3):
            term = jnp.dot(bank_ref[3 * dy + dx], planes[dy], preferred_element_type=jnp.float32)
            total = term if total is None else total + term
        sums.append(total)
    column = lax.broadcasted_iota(jnp.int32, sums[0].shape, 1) % cols
    left = jnp.where(column == 0, 0.0, pltpu.roll(sums[0], 1, 1))
    right = jnp.where(column == cols - 1, 0.0, pltpu.roll(sums[2], width - 1, 1))
    mixed = sums[1] + left + right + bias_ref[...]
    mixed = jnp.maximum(mixed, 0.0).astype(o_ref.dtype)
    for g in range(count):
        for row in range(rows_out):
            o_ref[g, row] = mixed[g * channels : (g + 1) * channels, row * cols : (row + 1) * cols]


def group_mix(bank, bias, windows, count, cols):
    full, wide = windows.shape
    channels = full // count
    rows_out = wide // cols - 2
    return pl.pallas_call(
        mixing_kernel,
        out_shape=jax.ShapeDtypeStruct((count, rows_out, channels, cols), jnp.bfloat16),
        compiler_params=pltpu.CompilerParams(vmem_limit_bytes=48 * 1024 * 1024),
    )(bank, bias, windows)


def layer(raster, coarse_features, lift_weight, lift_bias, group_weight, group_bias):
    n = lax.axis_size("rot")
    channels = lift_weight.shape[2]
    rows = raster.shape[1]

    tiles, cols = raster.shape[2], raster.shape[3]
    quarters = n // tiles
    span = rows // quarters
    space = lax.axis_index("space")

    lift_matrix = jnp.transpose(lift_weight[0], (1, 0, 2)).reshape(channels, -1)
    size = lax.axis_size("space")
    coarse_own = coarse_features[0]
    halo_shape = (-1,) + raster.shape[2:]

    def edges(raster_rows, coarse_row):
        return jnp.concatenate([raster_rows.reshape(halo_shape), coarse_row.reshape(halo_shape)], 0)

    up = [(i, i + 1) for i in range(size - 1)]
    from_above = lax.ppermute(edges(raster[:, rows - 2 :], coarse_own[:, rows - 1]), "space", up)
    from_below = lax.ppermute(edges(raster[:, :2], coarse_own[:, 0]), "space", [(j, i) for i, j in up])
    split_at = 2 * raster.shape[0]
    above = from_above[:split_at].reshape((-1, 2) + raster.shape[2:])
    below = from_below[:split_at].reshape((-1, 2) + raster.shape[2:])
    coarse_ext = jnp.concatenate(
        [from_above[split_at:][:, None], coarse_own, from_below[split_at:][:, None]], axis=1
    )

    def lift(source):
        count = source.shape[1] - 2
        widened = jnp.transpose(jnp.pad(source, ((0, 0), (0, 0), (0, 0), (1, 1))), (1, 2, 0, 3))
        taps = jnp.concatenate(
            [widened[dy : dy + count, :, :, dx : dx + cols] for dy in range(3) for dx in range(3)], 2
        )
        return jnp.einsum("ok,rtkw->rtow", lift_matrix, taps, preferred_element_type=jnp.float32)

    body = jnp.concatenate([above[:, 1:], raster, below[:, :1]], axis=1)
    first = jnp.concatenate([above, raster[:, :1]], axis=1)
    last = jnp.concatenate([raster[:, rows - 1 :], below], axis=1)
    lifted = jnp.concatenate([lift(first), lift(body), lift(last)], axis=0)
    coarse = jnp.transpose(coarse_ext, (1, 2, 0, 3))
    lifted = lifted + lift_bias[None, None, :, None] + coarse.astype(jnp.float32)
    line = lax.broadcasted_iota(jnp.int32, (rows + 2, 1, 1, 1), 0)
    inside = ((line > 0) | (space > 0)) & ((line < rows + 1) | (space < lax.axis_size("space") - 1))
    hidden_ext = jnp.where(inside, jnp.maximum(lifted, 0.0), 0.0).astype(jnp.bfloat16)

    split = (quarters, span) + hidden_ext.shape[1:]
    top = lax.slice_in_dim(hidden_ext, 0, rows, axis=0).reshape(split)
    bottom = lax.slice_in_dim(hidden_ext, 2, rows + 2, axis=0).reshape(split)
    windows = jnp.concatenate([top, lax.slice_in_dim(bottom, span - 2, span, axis=1)], axis=1)
    windows = jnp.transpose(windows, (2, 0, 3, 1, 4)).reshape((n, channels, (span + 2) * cols))
    gathered = lax.all_to_all(windows, "rot", 0, 0).reshape((n * channels, (span + 2) * cols))

    dense = group_weight[0].reshape(2, -1)
    spread = jnp.broadcast_to(dense, (n,) + dense.shape)
    filters = lax.all_to_all(spread, "rot", 0, 0)
    filters = filters.reshape((n,) + group_weight.shape[1:])
    bias = jnp.tile(group_bias, n)[:, None]
    mixed = group_mix(circulant_bank(filters), bias, gathered, n, cols)

    returned = lax.all_to_all(mixed, "rot", 0, 0)
    returned = returned.reshape((tiles, quarters) + returned.shape[1:])
    result = jnp.transpose(returned, (3, 1, 2, 0, 4)).reshape((channels, rows, tiles, cols))
    return result[None]


def solution(mesh):
    return jax.shard_map(
        layer,
        mesh=mesh,
        in_specs=(
            P(None, "space", None, None),
            P("rot", None, "space", None, None),
            P("rot", None, None, None),
            P(),
            P("rot", None, None, None),
            P(),
        ),
        out_specs=P("rot", None, "space", None, None),
        check_vma=False,
    )
```

```python
import jax
import jax.numpy as jnp
from jax import lax
from jax.experimental import pallas as pl
from jax.experimental.pallas import tpu as pltpu
from jax.sharding import PartitionSpec as P


def bank_kernel(pairs_ref, bank_ref):
    count, _, channels, lanes = pairs_ref.shape
    for g in range(count):
        for p in range(bank_ref.shape[2] // lanes):
            bank_ref[:, g * channels : (g + 1) * channels, p * lanes : (p + 1) * lanes] = pairs_ref[
                (g - 2 * p) % count
            ]


def circulant_bank(filters):
    count, taps, channels, _ = filters.shape
    pairs = jnp.concatenate([filters, jnp.roll(filters, 1, axis=0)], axis=-1)
    return pl.pallas_call(
        bank_kernel,
        out_shape=jax.ShapeDtypeStruct((taps, count * channels, count * channels), filters.dtype),
    )(pairs)


def mixing_kernel(bank_ref, bias_ref, x_ref, o_ref):
    count, rows_out, channels, cols = o_ref.shape
    planes = [
        jnp.concatenate([x_ref[row + dy] for row in range(rows_out)], axis=1) for dy in range(3)
    ]
    sums = []
    for dx in range(3):
        total = None
        for dy in range(3):
            term = jnp.dot(bank_ref[3 * dy + dx], planes[dy], preferred_element_type=jnp.float32)
            total = term if total is None else total + term
        sums.append(total)
    width = rows_out * cols
    column = lax.broadcasted_iota(jnp.int32, sums[0].shape, 1) % cols
    left = jnp.where(column == 0, 0.0, pltpu.roll(sums[0], 1, 1))
    right = jnp.where(column == cols - 1, 0.0, pltpu.roll(sums[2], width - 1, 1))
    mixed = sums[1] + left + right + bias_ref[...]
    mixed = jnp.maximum(mixed, 0.0).astype(o_ref.dtype)
    for g in range(count):
        for row in range(rows_out):
            o_ref[g, row] = mixed[g * channels : (g + 1) * channels, row * cols : (row + 1) * cols]


def group_mix(bank, bias, windows, count):
    rows_in, full, cols = windows.shape
    channels = full // count
    rows_out = rows_in - 2
    return pl.pallas_call(
        mixing_kernel,
        out_shape=jax.ShapeDtypeStruct((count, rows_out, channels, cols), jnp.bfloat16),
        compiler_params=pltpu.CompilerParams(vmem_limit_bytes=48 * 1024 * 1024),
    )(bank, bias, windows)


def layer(raster, coarse_features, lift_weight, lift_bias, group_weight, group_bias):
    n = lax.axis_size("rot")
    channels = lift_weight.shape[2]
    rows = raster.shape[1]

    tiles, cols = raster.shape[2], raster.shape[3]
    quarters = n // tiles
    span = rows // quarters
    space = lax.axis_index("space")

    lift_matrix = jnp.transpose(lift_weight[0], (1, 0, 2)).reshape(channels, -1)
    size = lax.axis_size("space")
    coarse_own = coarse_features[0]
    halo_shape = (-1,) + raster.shape[2:]

    def edges(raster_rows, coarse_row):
        return jnp.concatenate([raster_rows.reshape(halo_shape), coarse_row.reshape(halo_shape)], 0)

    up = [(i, i + 1) for i in range(size - 1)]
    from_above = lax.ppermute(edges(raster[:, rows - 2 :], coarse_own[:, rows - 1]), "space", up)
    from_below = lax.ppermute(edges(raster[:, :2], coarse_own[:, 0]), "space", [(j, i) for i, j in up])
    split_at = 2 * raster.shape[0]
    above = from_above[:split_at].reshape((-1, 2) + raster.shape[2:])
    below = from_below[:split_at].reshape((-1, 2) + raster.shape[2:])
    coarse_ext = jnp.concatenate(
        [from_above[split_at:][:, None], coarse_own, from_below[split_at:][:, None]], axis=1
    )

    def lift(source):
        count = source.shape[1] - 2
        widened = jnp.transpose(jnp.pad(source, ((0, 0), (0, 0), (0, 0), (1, 1))), (1, 2, 0, 3))
        taps = jnp.concatenate(
            [widened[dy : dy + count, :, :, dx : dx + cols] for dy in range(3) for dx in range(3)], 2
        )
        return jnp.einsum("ok,rtkw->rtow", lift_matrix, taps, preferred_element_type=jnp.float32)

    body = jnp.concatenate([above[:, 1:], raster, below[:, :1]], axis=1)
    first = jnp.concatenate([above, raster[:, :1]], axis=1)
    last = jnp.concatenate([raster[:, rows - 1 :], below], axis=1)
    lifted = jnp.concatenate([lift(first), lift(body), lift(last)], axis=0)
    coarse = jnp.transpose(coarse_ext, (1, 2, 0, 3))
    lifted = lifted + lift_bias[None, None, :, None] + coarse.astype(jnp.float32)
    line = lax.broadcasted_iota(jnp.int32, (rows + 2, 1, 1, 1), 0)
    inside = ((line > 0) | (space > 0)) & ((line < rows + 1) | (space < lax.axis_size("space") - 1))
    hidden_ext = jnp.where(inside, jnp.maximum(lifted, 0.0), 0.0).astype(jnp.bfloat16)

    split = (quarters, span) + hidden_ext.shape[1:]
    top = lax.slice_in_dim(hidden_ext, 0, rows, axis=0).reshape(split)
    bottom = lax.slice_in_dim(hidden_ext, 2, rows + 2, axis=0).reshape(split)
    windows = jnp.concatenate([top, lax.slice_in_dim(bottom, span - 2, span, axis=1)], axis=1)
    windows = jnp.transpose(windows, (2, 0, 1, 3, 4)).reshape((n, span + 2) + hidden_ext.shape[2:])
    gathered = lax.all_to_all(windows, "rot", 0, 1)
    gathered = gathered.reshape((gathered.shape[0], n * channels, cols))

    dense = group_weight[0].reshape(2, -1)
    spread = jnp.broadcast_to(dense, (n,) + dense.shape)
    filters = lax.all_to_all(spread, "rot", 0, 0)
    filters = filters.reshape((n,) + group_weight.shape[1:])
    bias = jnp.tile(group_bias, n)[:, None]
    mixed = group_mix(circulant_bank(filters), bias, gathered, n)

    returned = lax.all_to_all(mixed, "rot", 0, 0)
    returned = returned.reshape((tiles, quarters) + returned.shape[1:])
    result = jnp.transpose(returned, (3, 1, 2, 0, 4)).reshape((channels, rows, tiles, cols))
    return result[None]


def solution(mesh):
    return jax.shard_map(
        layer,
        mesh=mesh,
        in_specs=(
            P(None, "space", None, None),
            P("rot", None, "space", None, None),
            P("rot", None, None, None),
            P(),
            P("rot", None, None, None),
            P(),
        ),
        out_specs=P("rot", None, "space", None, None),
        check_vma=False,
    )
```
